128 devices in a mesh: req: 32 (over x, y, core), tp: 4 (over z).
Axes of the slice: x: 4, y: 4, z: 4, core: 2. Of those that a mesh axis runs over, the one named last changes fastest.
Arguments:
- stream: bfloat16 [64, 64, 3584], P('req'), may hold values from -40 to 40
- queries: bfloat16 [64, 64, 3584], P('req', None, 'tp'), may hold values from -4 to 4
- key_new: bfloat16 [64, 64, 3584], P('req', None, 'tp'), may hold values from -18 to 18
- value_new: bfloat16 [64, 64, 3584], P('req', None, 'tp'), may hold values from -6 to 6
- cache_key: bfloat16 [64, 1024, 3584], P('req', None, 'tp'), may hold values from -5 to 5
- cache_value: bfloat16 [64, 1024, 3584], P('req', None, 'tp'), may hold values from -6 to 6
- cache_length: int32 [64], P('req'), may hold values from 64 to 1024, as said below
- parents: int32 [64, 64], P('req'), may hold values from -1 to 62, as said below
- accept: int32 [64, 8, 64], P('req'), may hold values from 0 to 1, as said below
- out_weight: bfloat16 [3584, 3584], P('tp'), may hold values from -0.75 to 0.75
- norm_gain: float32 [3584], replicated, may hold values from 0.1 to 1.9
- head_weight: bfloat16 [32000, 3584], P('req'), may hold values from -1 to 1
- candidate: int32 [64, 64], replicated, may hold values from 0 to 31999
- dealing: int32 [64], replicated, may hold values from 0 to 63, each once
Outputs:
- target_logprob: float32 [64, 64], P('req')
- accepted_state: bfloat16 [64, 8, 3584], P('req', None, 'tp')
The draws below stay inside these ranges and needn't reach their ends.
Inputs may be any that keep to these rules, and one draw needn't show every extreme that they name: `cache_length`: every cache holds at least 64 live positions; in every draw some slot's cache is full. `parents`: node 0 is the root with parent -1; node t > 0 lies at depth (t - 1) // 9 + 1 and its parent lies one depth above it. `accept`: row a of a slot's matrix is one-hot on the node at depth a of the accepted path, which runs from the root down the slot's tree to some node; rows past the path's end are zero; in every draw some path ends at the deepest level.
All inputs are finite; a program needn't handle non-finite values.
Results may differ from the reference program's by a relative error of at most 0.012.
Values may be sent and summed in bfloat16 or wider, within the bound.
No kernel may reach another device: no remote copies, remote signals or barrier semaphores. Data moves between devices by JAX's collectives and lax.ppermute only.
A program may use at most 192 MiB of HBM per device.

```python
import math
import jax
import jax.numpy as jnp
import numpy as np
from jax import lax

D = 3584
HEADS = 16
HD = 224
VOCAB = 32000
CACHE = 1024
TREE = 64
ACC = 8
REQS = 64
QW = 3584


def feature_scale():
    return 0.1 * jnp.power(10.0, jnp.arange(D, dtype=jnp.float32) / D)


def draw_stream(key, part):
    row_scale = jnp.power(10.0, jax.random.uniform(jax.random.fold_in(key, 31), (REQS, TREE, 1), jnp.float32))
    values_base = jnp.clip(jax.random.normal(jax.random.fold_in(key, 32), (REQS, TREE, D), jnp.float32), -4.0, 4.0)
    return (values_base * row_scale * feature_scale()[None, None, :]).astype(jnp.bfloat16)


def draw_queries(key, part):
    values_base = jnp.clip(jax.random.normal(jax.random.fold_in(key, 42), (REQS, TREE, HEADS * HD), jnp.float32), -4.0, 4.0)
    return values_base.astype(jnp.bfloat16)


def draw_cache_key(key, part):
    values_base = jnp.clip(jax.random.normal(jax.random.fold_in(key, 43), (REQS, CACHE, HEADS * HD), jnp.float32), -4.0, 4.0)
    return values_base.astype(jnp.bfloat16)


def draw_head_weight(key, part):
    level = 3.0 / D ** 0.5
    values_base = jnp.clip(jax.random.normal(jax.random.fold_in(key, 44), (VOCAB, D), jnp.float32), -5.0, 5.0) * level
    return values_base.astype(jnp.bfloat16)


def draw_cache_length(key, part):
    halving = jax.random.randint(jax.random.fold_in(key, 51), (REQS,), 0, 4)
    trimmed = jax.random.randint(jax.random.fold_in(key, 52), (REQS,), 0, CACHE // 8)
    lengths = jnp.maximum(CACHE // jnp.left_shift(1, halving) - trimmed, TREE)
    full_slot = jax.random.randint(jax.random.fold_in(key, 53), (), 0, REQS)
    return jnp.where(jnp.arange(REQS) == full_slot, CACHE, lengths).astype(jnp.int32)


def tree_layout(key):
    node_ids = jnp.arange(TREE, dtype=jnp.int32)
    per_level = (TREE - 1) // (ACC - 1)
    depth = jnp.where(node_ids == 0, 0, (node_ids - 1) // per_level + 1)
    picks = jax.random.randint(jax.random.fold_in(key, 61), (REQS, TREE), 0, per_level)
    parents = jnp.where(depth == 0, -1, jnp.where(depth == 1, 0, 1 + (depth - 2) * per_level + picks))
    target = jax.random.randint(jax.random.fold_in(key, 62), (REQS,), 0, TREE)
    forced = jax.random.randint(jax.random.fold_in(key, 63), (), 0, REQS)
    target = jnp.where(jnp.arange(REQS) == forced, TREE - 1, target).astype(jnp.int32)
    chain_list = [target]
    current = target
    for hop_index in range(ACC - 1):
        current = jnp.maximum(jnp.take_along_axis(parents, current[:, None], axis=1)[:, 0], 0).astype(jnp.int32)
        chain_list.append(current)
    chain = jnp.stack(chain_list, axis=1)
    target_depth = depth[target]
    offsets = target_depth[:, None] - jnp.arange(ACC, dtype=jnp.int32)[None, :]
    node_at = jnp.take_along_axis(chain, jnp.clip(offsets, 0, ACC - 1), axis=1)
    hits = (node_at[:, :, None] == node_ids[None, None, :]) & (offsets >= 0)[:, :, None]
    return (parents.astype(jnp.int32), hits.astype(jnp.int32))


def draw_parents(key, part):
    return tree_layout(jax.random.fold_in(key, 60))[0]


def draw_accept(key, part):
    return tree_layout(jax.random.fold_in(key, 60))[1]


def plant(values, stream_key, low, largest):
    shape = values.shape
    place = [jax.random.randint(jax.random.fold_in(stream_key, axis), (), 0, shape[axis]) for axis in range(len(shape))]
    values = values.at[tuple(place)].set(low)
    longest = shape.index(max(shape))
    place[longest] = (place[longest] + 1) % shape[longest]
    return values.at[tuple(place)].set(largest)


def block_scale(key, shape, cuts, smallest, high):
    def one(position, shards_of):
        draws = jax.random.uniform(jax.random.fold_in(jax.random.fold_in(key, 6), position), (shards_of,), jnp.float32, smallest / len(cuts), high / len(cuts))
        return jnp.repeat(jnp.exp(draws), shape[position] // shards_of).reshape((-1,) + (1,) * (len(shape) - position - 1))

    factor_of = one(*cuts[0])
    for cut in cuts[1:]:
        factor_of = factor_of * one(*cut)
    return factor_of


def rank_bounds(count, slope):
    portions = [(1 << 20) // math.isqrt(rank ** slope) + 1 for rank in range(1, count + 1)]
    width = 1 + sum(portions) // (1 << 30)
    return np.cumsum(np.array([max(1, weight // width) for weight in portions]))


def ranked_ids(own_key, dims, count, slope):
    listing = rank_bounds(count, slope)
    lot = jax.random.randint(jax.random.fold_in(own_key, 1), dims, 0, int(listing[count - 1]))
    grade = jnp.searchsorted(jnp.asarray(listing, jnp.int32), lot, side="right")
    return jax.random.permutation(jax.random.fold_in(own_key, 2), count)[grade].astype(jnp.int32)


def noise(key, dims, spread, bound, shards=(), kind=jnp.bfloat16):
    gain = block_scale(key, dims, shards, -0.22, 0.18) if shards else 1.0
    drawn = jax.random.normal(key, dims, jnp.float32) * spread * gain
    return jnp.minimum(jnp.maximum(drawn, -bound), bound).astype(kind)


def setup_inputs(seed: int = 0) -> dict:
    keys = jax.random.split(jax.random.key(seed), 15)
    stream = draw_stream(jax.random.fold_in(keys[14], 71), 0)
    queries = draw_queries(jax.random.fold_in(keys[14], 71), 0)
    key_new = noise(keys[2], (REQS, TREE, QW), 3.0, 18.0, ((0, 32), (2, 4)))
    value_new = noise(keys[3], (REQS, TREE, QW), 1.0, 6.0, ((0, 32), (2, 4)))
    cache_key = draw_cache_key(jax.random.fold_in(keys[14], 71), 0)
    cache_value = noise(keys[5], (REQS, CACHE, QW), 1.0, 6.0, ((0, 32), (2, 4)))
    cache_length = draw_cache_length(jax.random.fold_in(keys[14], 71), 0)
    parents = draw_parents(jax.random.fold_in(keys[14], 71), 0)
    accept = draw_accept(jax.random.fold_in(keys[14], 71), 0)
    out_weight = noise(keys[9], (QW, D), (HEADS * HD // 64) ** -0.5, 0.75, ((0, 4),))
    norm_gain = jnp.clip(1.0 + 0.18 * jax.random.normal(keys[10], (D,), jnp.float32), 0.1, 1.9)
    head_weight = draw_head_weight(jax.random.fold_in(keys[14], 71), 0)
    candidate = plant(ranked_ids(keys[12], (REQS, TREE), VOCAB, 2), jax.random.fold_in(keys[12], 3), 0, VOCAB - 1).astype(jnp.int32)
    dealing = jax.random.permutation(keys[13], REQS).astype(jnp.int32)
    return dict(stream=stream, queries=queries, key_new=key_new, value_new=value_new, cache_key=cache_key, cache_value=cache_value, cache_length=cache_length, parents=parents, accept=accept, out_weight=out_weight, norm_gain=norm_gain, head_weight=head_weight, candidate=candidate, dealing=dealing)


EPS = 1e-05
HIGH = lax.Precision.HIGHEST

def ancestry(parents):
    node_count = parents.shape[-1]
    node_ids = jnp.arange(node_count, dtype=jnp.int32)
    stride_map = (parents[..., :, None] == node_ids).astype(jnp.float32)
    reached = jnp.broadcast_to(jnp.eye(node_count, dtype=jnp.float32), stride_map.shape)
    for doubling in range((ACC - 1).bit_length()):
        reached = reached + jnp.einsum('rtk,rku->rtu', reached, stride_map, precision=HIGH)
        stride_map = jnp.einsum('rtk,rku->rtu', stride_map, stride_map, precision=HIGH)
    return reached > 0.5

def rounded_weights(values):
    return lax.optimization_barrier(values.astype(jnp.bfloat16)).astype(jnp.float32)

def reference(stream, queries, key_new, value_new, cache_key, cache_value, cache_length, parents, accept, out_weight, norm_gain, head_weight, candidate, dealing):
    visible = ancestry(parents)
    factor = HD ** (-0.5)

    def attend(members):
        query_rows, tree_keys, tree_values, past_keys, past_values, live_count, seen = members
        query_rows = query_rows.astype(jnp.float32).reshape(TREE, HEADS, HD)
        past_keys = past_keys.astype(jnp.float32).reshape(CACHE, HEADS, HD)
        past_values = past_values.astype(jnp.float32).reshape(CACHE, HEADS, HD)
        tree_keys = tree_keys.astype(jnp.float32).reshape(TREE, HEADS, HD)
        tree_values = tree_values.astype(jnp.float32).reshape(TREE, HEADS, HD)
        positions = jnp.arange(CACHE, dtype=jnp.int32)
        past_scores = jnp.einsum('thd,khd->htk', query_rows, past_keys) * factor
        past_scores = jnp.where((positions < live_count)[None, None, :], past_scores, -jnp.inf)
        tree_scores = jnp.einsum('thd,khd->htk', query_rows, tree_keys) * factor
        tree_scores = jnp.where(seen[None], tree_scores, -jnp.inf)
        highest = jnp.maximum(lax.optimization_barrier(jnp.max(past_scores, axis=2)), lax.optimization_barrier(jnp.max(tree_scores, axis=2)))
        past_weights = jnp.exp(past_scores - highest[..., None])
        tree_weights = jnp.exp(tree_scores - highest[..., None])
        denominator = lax.optimization_barrier(jnp.sum(past_weights, axis=2)) + lax.optimization_barrier(jnp.sum(tree_weights, axis=2))
        mixed = jnp.einsum('htk,khd->htd', rounded_weights(past_weights), past_values)
        mixed = mixed + jnp.einsum('htk,khd->htd', rounded_weights(tree_weights), tree_values)
        mixed = mixed / denominator[..., None]
        return mixed.transpose(1, 0, 2).reshape(TREE, HEADS * HD).astype(jnp.bfloat16)
    attention = lax.map(attend, (queries, key_new, value_new, cache_key, cache_value, cache_length, visible))
    projected = jnp.dot(attention.reshape(REQS * TREE, HEADS * HD), out_weight, preferred_element_type=jnp.float32)
    post_rows = (stream.reshape(REQS * TREE, D).astype(jnp.float32) + projected).astype(jnp.bfloat16)
    post_float = post_rows.astype(jnp.float32)
    inverse = lax.rsqrt(lax.optimization_barrier(jnp.mean(post_float * post_float, axis=1, keepdims=True)) + EPS)
    normed = (post_float * inverse * norm_gain.astype(jnp.float32)[None, :]).astype(jnp.bfloat16)

    def head_block(members):
        block_rows, block_ids = members
        logits = lax.dot_general(block_rows, head_weight, (((1,), (1,)), ((), ())), preferred_element_type=jnp.float32)
        highest = lax.optimization_barrier(jnp.max(logits, axis=1))
        summed = lax.optimization_barrier(jnp.sum(jnp.exp(logits - highest[:, None]), axis=1))
        words = jnp.arange(VOCAB, dtype=jnp.int32)
        picked = lax.optimization_barrier(jnp.sum(jnp.where(words[None, :] == block_ids[:, None], logits, 0.0), axis=1))
        return picked - highest - jnp.log(summed)
    block_size = 512
    slot_logprob = lax.map(head_block, (normed.reshape(-1, block_size, D), candidate.reshape(-1, block_size))).reshape(REQS, TREE)
    reorder = (dealing[None, :] == jnp.arange(REQS, dtype=jnp.int32)[:, None]).astype(jnp.float32)
    target_logprob = jnp.dot(reorder, slot_logprob, precision=HIGH)
    compact = jnp.einsum('sat,std->sad', accept.astype(jnp.float32), post_float.reshape(REQS, TREE, D), precision=HIGH)
    accepted_state = jnp.einsum('rs,sad->rad', reorder, compact, precision=HIGH).astype(jnp.bfloat16)
    return (target_logprob, accepted_state)
```

```python
import jax
import jax.numpy as jnp
from jax import lax
from jax.sharding import PartitionSpec as P

HD = 224
ACC = 8


EPS = 1e-05
HIGH = lax.Precision.HIGHEST
block_limit = 512


def combined_all(value, axis, join):
    pieces = jax.tree.map(lambda part: lax.all_gather(part, axis), value)
    head = jax.tree.map(lambda part: part[0], pieces)
    tail = jax.tree.map(lambda part: part[1:], pieces)
    subtotal, _ = lax.scan(lambda subtotal, share: (join(subtotal, share), None), head, tail)
    return subtotal


def ancestry(parents):
    node_count = parents.shape[-1]
    node_ids = jnp.arange(node_count, dtype=jnp.int32)
    stride_map = (parents[..., :, None] == node_ids).astype(jnp.float32)
    reached = jnp.broadcast_to(jnp.eye(node_count, dtype=jnp.float32), stride_map.shape) > 0.5
    for doubling in range((ACC - 1).bit_length()):
        further = lax.optimization_barrier(
            jnp.einsum("rtk,rku->rtu", reached.astype(jnp.float32), stride_map, precision=HIGH)
        )
        reached = jnp.logical_or(reached, further > 0.5)
        stride_map = jnp.einsum("rtk,rku->rtu", stride_map, stride_map, precision=HIGH)
    return reached


def combine_stats(earlier, later):
    joint_max = jnp.maximum(earlier[0], later[0])
    joint_sum = earlier[1] * jnp.exp(earlier[0] - joint_max) + later[1] * jnp.exp(
        later[0] - joint_max
    )
    return (joint_max, joint_sum, earlier[2] + later[2])


def vocab_stats(logits, vocab_ids, wanted, along):
    row_max = jnp.max(logits, axis=along)
    row_sum = jnp.sum(jnp.exp(logits - jnp.expand_dims(row_max, along)), axis=along)
    matches = jnp.expand_dims(vocab_ids, 1 - along) == jnp.expand_dims(wanted, along)
    picked = jnp.sum(jnp.where(matches, logits, 0.0), axis=along)
    return (row_max, row_sum, picked)


def local(
    stream,
    queries,
    key_new,
    value_new,
    cache_key,
    cache_value,
    cache_length,
    parents,
    accept,
    out_weight,
    norm_gain,
    head_weight,
    candidate,
    dealing,
):
    slots, tree_size, qwidth = queries.shape
    model_width = stream.shape[2]
    heads_loc = qwidth // HD
    n_tp = lax.axis_size("tp")
    n_req = lax.axis_size("req")
    tp_id = lax.axis_index("tp")
    req_id = lax.axis_index("req")
    score_scale = HD ** (-0.5)
    query_rows = queries.reshape(slots, tree_size, heads_loc, HD)
    tree_keys = key_new.reshape(slots, tree_size, heads_loc, HD)
    tree_values = value_new.reshape(slots, tree_size, heads_loc, HD)
    visible = ancestry(parents)
    tree_scores = (
        jnp.einsum("rthd,rkhd->rhtk", query_rows, tree_keys, preferred_element_type=jnp.float32)
        * score_scale
    )
    tree_scores = jnp.where(visible[:, None], tree_scores, -jnp.inf)
    running_max = jnp.max(tree_scores, axis=3)
    weights = jnp.exp(tree_scores - running_max[..., None])
    running_sum = jnp.sum(weights, axis=3)
    running_out = jnp.einsum(
        "rhtk,rkhd->rhtd",
        weights.astype(jnp.bfloat16),
        tree_values,
        preferred_element_type=jnp.float32,
    )
    cache_cap = cache_key.shape[1]
    block_rows = min(block_limit, cache_cap)
    block_count = (jnp.max(cache_length) + block_rows - 1) // block_rows

    def visit_block(block_index, folded):
        old_max, old_sum, old_out = folded
        offset = block_index * block_rows
        past_keys = lax.dynamic_slice_in_dim(cache_key, offset, block_rows, 1).reshape(
            slots, block_rows, heads_loc, HD
        )
        past_values = lax.dynamic_slice_in_dim(cache_value, offset, block_rows, 1).reshape(
            slots, block_rows, heads_loc, HD
        )
        scores = (
            jnp.einsum("rthd,rkhd->rhtk", query_rows, past_keys, preferred_element_type=jnp.float32)
            * score_scale
        )
        live_mask = (offset + jnp.arange(block_rows, dtype=jnp.int32))[None, :] < cache_length[
            :, None
        ]
        scores = jnp.where(live_mask[:, None, None, :], scores, -jnp.inf)
        new_max = jnp.maximum(old_max, jnp.max(scores, axis=3))
        shrink = jnp.exp(old_max - new_max)
        block_weights = jnp.exp(scores - new_max[..., None])
        new_sum = old_sum * shrink + jnp.sum(block_weights, axis=3)
        contribution = lax.optimization_barrier(
            jnp.einsum(
                "rhtk,rkhd->rhtd",
                block_weights.astype(jnp.bfloat16),
                past_values,
                preferred_element_type=jnp.float32,
            )
        )
        new_out = old_out * shrink[..., None] + contribution
        return (new_max, new_sum, new_out)

    running_max, running_sum, running_out = lax.fori_loop(
        0, block_count, visit_block, (running_max, running_sum, running_out)
    )
    attention = (running_out / running_sum[..., None]).astype(jnp.bfloat16)
    attention_rows = attention.transpose(0, 2, 1, 3).reshape(slots * tree_size, qwidth)
    rows_all = slots * tree_size
    quarter = rows_all // n_tp
    dslice = model_width // n_tp
    acc_rows = accept.shape[1]
    partial_out = jnp.dot(
        attention_rows, out_weight, preferred_element_type=jnp.float32
    ).astype(jnp.bfloat16)
    accept_b = accept.astype(jnp.bfloat16)
    partial_compact = jnp.einsum(
        "sat,std->sad",
        accept_b,
        partial_out.reshape(slots, tree_size, model_width),
        preferred_element_type=jnp.float32,
    ).astype(jnp.bfloat16)
    compact_pieces = (
        partial_compact.reshape(slots * acc_rows, n_tp, dslice)
        .transpose(1, 0, 2)
        .reshape(n_tp * slots * acc_rows, dslice)
    )
    summed = lax.psum_scatter(partial_out, "tp", scatter_dimension=0, tiled=True).astype(
        jnp.float32
    )
    summed_compact = lax.psum_scatter(
        compact_pieces, "tp", scatter_dimension=0, tiled=True
    ).astype(jnp.float32)
    flat_stream = stream.reshape(rows_all, model_width)
    own_stream = lax.dynamic_slice_in_dim(flat_stream, tp_id * quarter, quarter, 0)
    post_rows = (own_stream.astype(jnp.float32) + summed).astype(jnp.bfloat16)
    post_float = post_rows.astype(jnp.float32)
    square = jnp.sum(post_float * post_float, axis=1)
    inverse = lax.rsqrt(square / model_width + EPS)
    normed = (post_float * inverse[:, None] * norm_gain[None, :]).astype(jnp.bfloat16)
    stream_pick = jnp.einsum(
        "sat,std->sad", accept_b, stream, preferred_element_type=jnp.float32
    )
    stream_pick = lax.dynamic_slice_in_dim(stream_pick, tp_id * dslice, dslice, 2)
    compact = (
        stream_pick + summed_compact.reshape(slots, acc_rows, dslice)
    ).astype(jnp.bfloat16)
    extra = slots * acc_rows * dslice // model_width
    payload = jnp.concatenate(
        [normed, compact.reshape(extra, model_width)], axis=0
    )
    gathered = lax.all_gather(payload, "req", axis=0, tiled=True).reshape(
        n_req, quarter + extra, model_width
    )
    all_rows = gathered[:, :quarter].reshape(n_req * quarter, model_width)
    vocab_loc = head_weight.shape[0]
    wanted_rows = lax.dynamic_slice_in_dim(
        candidate.reshape(n_req, rows_all), tp_id * quarter, quarter, 1
    ).reshape(-1)
    vocab_ids = req_id * vocab_loc + jnp.arange(vocab_loc, dtype=jnp.int32)
    logits = lax.dot_general(
        all_rows, head_weight, (((1,), (1,)), ((), ())), preferred_element_type=jnp.float32
    )
    row_max, row_sum, picked = vocab_stats(logits, vocab_ids, wanted_rows, 1)
    stats = lax.all_gather(jnp.stack([row_max, row_sum, picked]), "req", axis=0)
    joint_max = jnp.max(stats[:, 0], axis=0)
    joint_sum = jnp.sum(stats[:, 1] * jnp.exp(stats[:, 0] - joint_max[None]), axis=0)
    joint_pick = jnp.sum(stats[:, 2], axis=0)
    plane_logprob = joint_pick - joint_max - jnp.log(joint_sum)
    every = lax.all_gather(plane_logprob, "tp", axis=0)
    logprob = (
        every.reshape(n_tp // 2, 2, n_req, quarter)
        .transpose(2, 0, 1, 3)
        .reshape(n_req * slots, tree_size)
    )
    own_requests = req_id * slots + jnp.arange(slots, dtype=jnp.int32)
    selector = dealing[None, :] == own_requests[:, None]
    target_logprob = jnp.dot(selector.astype(jnp.float32), logprob, precision=HIGH)
    home_states = gathered[:, quarter:].reshape(n_req * slots, acc_rows, dslice)
    accepted_state = jnp.einsum(
        "ks,sad->kad",
        selector.astype(jnp.bfloat16),
        home_states,
        preferred_element_type=jnp.float32,
    ).astype(jnp.bfloat16)
    return (target_logprob, accepted_state)


def solution(mesh):
    placed = (
        P("req", None, None),
        P("req", None, "tp"),
        P("req", None, "tp"),
        P("req", None, "tp"),
        P("req", None, "tp"),
        P("req", None, "tp"),
        P("req"),
        P("req", None),
        P("req", None, None),
        P("tp", None),
        P(),
        P("req", None),
        P(),
        P(),
    )
    return jax.shard_map(
        local,
        mesh=mesh,
        in_specs=placed,
        out_specs=(P("req", None), P("req", None, "tp")),
        check_vma=False,
    )
```

```python
import jax
import jax.numpy as jnp
from jax import lax
from jax.sharding import PartitionSpec as P

HD = 224
ACC = 8


EPS = 1e-05
HIGH = lax.Precision.HIGHEST
block_limit = 512


def combined_all(value, axis, join):
    pieces = jax.tree.map(lambda part: lax.all_gather(part, axis), value)
    head = jax.tree.map(lambda part: part[0], pieces)
    tail = jax.tree.map(lambda part: part[1:], pieces)
    subtotal, _ = lax.scan(lambda subtotal, share: (join(subtotal, share), None), head, tail)
    return subtotal


def ancestry(parents):
    node_count = parents.shape[-1]
    node_ids = jnp.arange(node_count, dtype=jnp.int32)
    stride_map = (parents[..., :, None] == node_ids).astype(jnp.float32)
    reached = jnp.broadcast_to(jnp.eye(node_count, dtype=jnp.float32), stride_map.shape) > 0.5
    for doubling in range((ACC - 1).bit_length()):
        further = lax.optimization_barrier(
            jnp.einsum("rtk,rku->rtu", reached.astype(jnp.float32), stride_map, precision=HIGH)
        )
        reached = jnp.logical_or(reached, further > 0.5)
        stride_map = jnp.einsum("rtk,rku->rtu", stride_map, stride_map, precision=HIGH)
    return reached


def combine_stats(earlier, later):
    joint_max = jnp.maximum(earlier[0], later[0])
    joint_sum = earlier[1] * jnp.exp(earlier[0] - joint_max) + later[1] * jnp.exp(
        later[0] - joint_max
    )
    return (joint_max, joint_sum, earlier[2] + later[2])


def vocab_stats(logits, vocab_ids, wanted, along):
    row_max = jnp.max(logits, axis=along)
    row_sum = jnp.sum(jnp.exp(logits - jnp.expand_dims(row_max, along)), axis=along)
    matches = jnp.expand_dims(vocab_ids, 1 - along) == jnp.expand_dims(wanted, along)
    picked = jnp.sum(jnp.where(matches, logits, 0.0), axis=along)
    return (row_max, row_sum, picked)


def local(
    stream,
    queries,
    key_new,
    value_new,
    cache_key,
    cache_value,
    cache_length,
    parents,
    accept,
    out_weight,
    norm_gain,
    head_weight,
    candidate,
    dealing,
):
    slots, tree_size, qwidth = queries.shape
    model_width = stream.shape[2]
    heads_loc = qwidth // HD
    n_tp = lax.axis_size("tp")
    n_req = lax.axis_size("req")
    tp_id = lax.axis_index("tp")
    req_id = lax.axis_index("req")
    score_scale = HD ** (-0.5)
    cache_cap = cache_key.shape[1]
    column_head = jnp.arange(qwidth, dtype=jnp.int32) // HD
    head_mask = column_head[None, :] == jnp.arange(heads_loc, dtype=jnp.int32)[:, None]
    spread_q = jnp.where(
        head_mask[None, :, None, :], queries[:, None, :, :], jnp.zeros((), queries.dtype)
    ).reshape(slots, heads_loc * tree_size, qwidth)
    past_scores = (
        jnp.einsum("rnd,rkd->rnk", spread_q, cache_key, preferred_element_type=jnp.float32)
        * score_scale
    )
    live = jnp.arange(cache_cap, dtype=jnp.int32)[None, :] < cache_length[:, None]
    past_scores = jnp.where(live[:, None, :], past_scores, -jnp.inf)
    visible = ancestry(parents)
    seen = jnp.broadcast_to(
        visible[:, None], (slots, heads_loc, tree_size, tree_size)
    ).reshape(slots, heads_loc * tree_size, tree_size)
    tree_scores = (
        jnp.einsum("rnd,rkd->rnk", spread_q, key_new, preferred_element_type=jnp.float32)
        * score_scale
    )
    tree_scores = jnp.where(seen, tree_scores, -jnp.inf)
    highest = jnp.maximum(jnp.max(past_scores, axis=2), jnp.max(tree_scores, axis=2))
    past_weights = jnp.exp(past_scores - highest[..., None])
    tree_weights = jnp.exp(tree_scores - highest[..., None])
    denominator = jnp.sum(past_weights, axis=2) + jnp.sum(tree_weights, axis=2)
    mixed = jnp.einsum(
        "rnk,rkd->rnd",
        past_weights.astype(jnp.bfloat16),
        cache_value,
        preferred_element_type=jnp.float32,
    ) + jnp.einsum(
        "rnk,rkd->rnd",
        tree_weights.astype(jnp.bfloat16),
        value_new,
        preferred_element_type=jnp.float32,
    )
    mixed = (mixed / denominator[..., None]).reshape(slots, heads_loc, tree_size, qwidth)
    attention = jnp.sum(
        jnp.where(head_mask[None, :, None, :], mixed, 0.0), axis=1
    ).astype(jnp.bfloat16)
    attention_rows = attention.reshape(slots * tree_size, qwidth)
    rows_all = slots * tree_size
    quarter = rows_all // n_tp
    dslice = model_width // n_tp
    halves = tree_size // quarter
    acc_rows = accept.shape[1]
    own_slot = tp_id // halves
    node_off = (tp_id % halves) * quarter
    partial_out = jnp.dot(
        attention_rows, out_weight, preferred_element_type=jnp.float32
    ).astype(jnp.bfloat16)
    summed = lax.psum_scatter(partial_out, "tp", scatter_dimension=0, tiled=True).astype(
        jnp.float32
    )
    flat_stream = stream.reshape(rows_all, model_width)
    own_stream = lax.dynamic_slice_in_dim(flat_stream, tp_id * quarter, quarter, 0)
    post_rows = (own_stream.astype(jnp.float32) + summed).astype(jnp.bfloat16)
    post_float = post_rows.astype(jnp.float32)
    square = jnp.sum(post_float * post_float, axis=1)
    inverse = lax.rsqrt(square / model_width + EPS)
    normed = (post_float * inverse[:, None] * norm_gain[None, :]).astype(jnp.bfloat16)
    accept_own = lax.dynamic_slice_in_dim(
        lax.dynamic_index_in_dim(accept, own_slot, 0, keepdims=False), node_off, quarter, 1
    )
    picked_rows = jnp.dot(
        accept_own.astype(jnp.bfloat16), post_rows, preferred_element_type=jnp.float32
    ).astype(jnp.bfloat16)
    payload = jnp.concatenate([normed, picked_rows], axis=0)
    gathered = lax.all_gather(payload, "req", axis=0, tiled=True).reshape(
        n_req, quarter + acc_rows, model_width
    )
    all_rows = gathered[:, :quarter].reshape(n_req * quarter, model_width)
    vocab_loc = head_weight.shape[0]
    wanted_rows = lax.dynamic_slice_in_dim(
        candidate.reshape(n_req, rows_all), tp_id * quarter, quarter, 1
    ).reshape(-1)
    vocab_ids = req_id * vocab_loc + jnp.arange(vocab_loc, dtype=jnp.int32)
    logits = lax.dot_general(
        all_rows, head_weight, (((1,), (1,)), ((), ())), preferred_element_type=jnp.float32
    )
    row_max, row_sum, picked = vocab_stats(logits, vocab_ids, wanted_rows, 1)
    stats = lax.all_gather(jnp.stack([row_max, row_sum, picked]), "req", axis=0)
    joint_max = jnp.max(stats[:, 0], axis=0)
    joint_sum = jnp.sum(stats[:, 1] * jnp.exp(stats[:, 0] - joint_max[None]), axis=0)
    joint_pick = jnp.sum(stats[:, 2], axis=0)
    plane_logprob = (joint_pick - joint_max - jnp.log(joint_sum)).reshape(n_req, quarter)
    own_requests = req_id * slots + jnp.arange(slots, dtype=jnp.int32)
    slot_ids = jnp.arange(dealing.shape[0], dtype=jnp.int32)
    serving = jnp.sum(
        jnp.where(dealing[None, :] == own_requests[:, None], slot_ids[None, :], 0), axis=1
    )
    source = serving // slots
    held = (serving % slots) == own_slot
    lp_rows = jnp.take(plane_logprob, source, axis=0)
    node_half = jnp.arange(tree_size, dtype=jnp.int32) // quarter == tp_id % halves
    lp_full = jnp.where(
        held[:, None] & node_half[None, :], jnp.tile(lp_rows, (1, halves)), 0.0
    )
    state_rows = jnp.take(gathered[:, quarter:], source, axis=0).astype(jnp.float32)
    state_rows = jnp.where(held[:, None, None], state_rows, 0.0)
    state_parts = state_rows.reshape(slots * acc_rows, n_tp, dslice).transpose(1, 0, 2)
    outgoing = jnp.concatenate(
        [
            state_parts.reshape(n_tp, slots * acc_rows * dslice),
            jnp.broadcast_to(lp_full.reshape(1, -1), (n_tp, slots * tree_size)),
        ],
        axis=1,
    )
    incoming = lax.all_to_all(outgoing, "tp", split_axis=0, concat_axis=0, tiled=True)
    merged = jnp.sum(incoming, axis=0)
    accepted_state = (
        merged[: slots * acc_rows * dslice].reshape(slots, acc_rows, dslice).astype(jnp.bfloat16)
    )
    target_logprob = merged[slots * acc_rows * dslice :].reshape(slots, tree_size)
    return (target_logprob, accepted_state)


def solution(mesh):
    placed = (
        P("req", None, None),
        P("req", None, "tp"),
        P("req", None, "tp"),
        P("req", None, "tp"),
        P("req", None, "tp"),
        P("req", None, "tp"),
        P("req"),
        P("req", None),
        P("req", None, None),
        P("tp", None),
        P(),
        P("req", None),
        P(),
        P(),
    )
    return jax.shard_map(
        local,
        mesh=mesh,
        in_specs=placed,
        out_specs=(P("req", None), P("req", None, "tp")),
        check_vma=False,
    )
```

```python
import jax
import jax.numpy as jnp
from jax import lax
from jax.sharding import PartitionSpec as P

HD = 224
ACC = 8


EPS = 1e-05
HIGH = lax.Precision.HIGHEST
block_limit = 512


def combined_all(value, axis, join):
    pieces = jax.tree.map(lambda part: lax.all_gather(part, axis), value)
    head = jax.tree.map(lambda part: part[0], pieces)
    tail = jax.tree.map(lambda part: part[1:], pieces)
    subtotal, _ = lax.scan(lambda subtotal, share: (join(subtotal, share), None), head, tail)
    return subtotal


def ancestry(parents):
    node_count = parents.shape[-1]
    node_ids = jnp.arange(node_count, dtype=jnp.int32)
    stride_map = (parents[..., :, None] == node_ids).astype(jnp.float32)
    reached = jnp.broadcast_to(jnp.eye(node_count, dtype=jnp.float32), stride_map.shape) > 0.5
    for doubling in range((ACC - 1).bit_length()):
        further = lax.optimization_barrier(
            jnp.einsum("rtk,rku->rtu", reached.astype(jnp.float32), stride_map, precision=HIGH)
        )
        reached = jnp.logical_or(reached, further > 0.5)
        stride_map = jnp.einsum("rtk,rku->rtu", stride_map, stride_map, precision=HIGH)
    return reached


def combine_stats(earlier, later):
    joint_max = jnp.maximum(earlier[0], later[0])
    joint_sum = earlier[1] * jnp.exp(earlier[0] - joint_max) + later[1] * jnp.exp(
        later[0] - joint_max
    )
    return (joint_max, joint_sum, earlier[2] + later[2])


def vocab_stats(logits, vocab_ids, wanted, along):
    row_max = jnp.max(logits, axis=along)
    row_sum = jnp.sum(jnp.exp(logits - jnp.expand_dims(row_max, along)), axis=along)
    matches = jnp.expand_dims(vocab_ids, 1 - along) == jnp.expand_dims(wanted, along)
    picked = jnp.sum(jnp.where(matches, logits, 0.0), axis=along)
    return (row_max, row_sum, picked)


def local(
    stream,
    queries,
    key_new,
    value_new,
    cache_key,
    cache_value,
    cache_length,
    parents,
    accept,
    out_weight,
    norm_gain,
    head_weight,
    candidate,
    dealing,
):
    slots, tree_size, qwidth = queries.shape
    model_width = stream.shape[2]
    heads_loc = qwidth // HD
    n_tp = lax.axis_size("tp")
    n_req = lax.axis_size("req")
    tp_id = lax.axis_index("tp")
    req_id = lax.axis_index("req")
    score_scale = HD ** (-0.5)
    cache_cap = cache_key.shape[1]
    column_head = jnp.arange(qwidth, dtype=jnp.int32) // HD
    head_mask = column_head[None, :] == jnp.arange(heads_loc, dtype=jnp.int32)[:, None]
    spread_q = jnp.where(
        head_mask[None, :, None, :], queries[:, None, :, :], jnp.zeros((), queries.dtype)
    ).reshape(slots, heads_loc * tree_size, qwidth)
    past_scores = (
        jnp.einsum("rnd,rkd->rnk", spread_q, cache_key, preferred_element_type=jnp.float32)
        * score_scale
    )
    live = jnp.arange(cache_cap, dtype=jnp.int32)[None, :] < cache_length[:, None]
    past_scores = jnp.where(live[:, None, :], past_scores, -jnp.inf)
    visible = ancestry(parents)
    seen = jnp.broadcast_to(
        visible[:, None], (slots, heads_loc, tree_size, tree_size)
    ).reshape(slots, heads_loc * tree_size, tree_size)
    tree_scores = (
        jnp.einsum("rnd,rkd->rnk", spread_q, key_new, preferred_element_type=jnp.float32)
        * score_scale
    )
    tree_scores = jnp.where(seen, tree_scores, -jnp.inf)
    highest = jnp.maximum(jnp.max(past_scores, axis=2), jnp.max(tree_scores, axis=2))
    past_weights = jnp.exp(past_scores - highest[..., None])
    tree_weights = jnp.exp(tree_scores - highest[..., None])
    denominator = jnp.sum(past_weights, axis=2) + jnp.sum(tree_weights, axis=2)
    mixed = jnp.einsum(
        "rnk,rkd->rnd",
        past_weights.astype(jnp.bfloat16),
        cache_value,
        preferred_element_type=jnp.float32,
    ) + jnp.einsum(
        "rnk,rkd->rnd",
        tree_weights.astype(jnp.bfloat16),
        value_new,
        preferred_element_type=jnp.float32,
    )
    mixed = (mixed / denominator[..., None]).reshape(slots, heads_loc, tree_size, qwidth)
    attention = jnp.sum(
        jnp.where(head_mask[None, :, None, :], mixed, 0.0), axis=1
    ).astype(jnp.bfloat16)
    attention_rows = attention.reshape(slots * tree_size, qwidth)
    rows_all = slots * tree_size
    quarter = rows_all // n_tp
    dslice = model_width // n_tp
    halves = tree_size // quarter
    acc_rows = accept.shape[1]
    own_slot = tp_id // halves
    node_off = (tp_id % halves) * quarter
    partial_out = jnp.dot(
        attention_rows, out_weight, preferred_element_type=jnp.float32
    ).astype(jnp.bfloat16)
    arriving = lax.all_to_all(
        partial_out.reshape(n_tp, quarter, model_width), "tp", split_axis=0, concat_axis=0, tiled=True
    )
    summed = jnp.sum(arriving.astype(jnp.float32), axis=0)
    flat_stream = stream.reshape(rows_all, model_width)
    own_stream = lax.dynamic_slice_in_dim(flat_stream, tp_id * quarter, quarter, 0)
    post_rows = (own_stream.astype(jnp.float32) + summed).astype(jnp.bfloat16)
    post_float = post_rows.astype(jnp.float32)
    square = jnp.sum(post_float * post_float, axis=1)
    inverse = lax.rsqrt(square / model_width + EPS)
    normed = (post_float * inverse[:, None] * norm_gain[None, :]).astype(jnp.bfloat16)
    accept_own = lax.dynamic_slice_in_dim(
        lax.dynamic_index_in_dim(accept, own_slot, 0, keepdims=False), node_off, quarter, 1
    )
    picked_rows = jnp.dot(
        accept_own.astype(jnp.bfloat16), post_rows, preferred_element_type=jnp.float32
    ).astype(jnp.bfloat16)
    payload = jnp.concatenate([normed, picked_rows], axis=0)
    gathered = lax.all_gather(payload, "req", axis=0, tiled=True).reshape(
        n_req, quarter + acc_rows, model_width
    )
    all_rows = gathered.reshape(n_req * (quarter + acc_rows), model_width)
    vocab_loc = head_weight.shape[0]
    wanted_rows = jnp.concatenate(
        [
            lax.dynamic_slice_in_dim(
                candidate.reshape(n_req, rows_all), tp_id * quarter, quarter, 1
            ),
            jnp.zeros((n_req, acc_rows), candidate.dtype),
        ],
        axis=1,
    ).reshape(-1)
    vocab_ids = req_id * vocab_loc + jnp.arange(vocab_loc, dtype=jnp.int32)
    logits = lax.dot_general(
        all_rows, head_weight, (((1,), (1,)), ((), ())), preferred_element_type=jnp.float32
    )
    row_max, row_sum, picked = vocab_stats(logits, vocab_ids, wanted_rows, 1)
    local_stats = jnp.stack([row_max, row_sum, picked]).reshape(3, n_req, quarter + acc_rows)
    local_stats = local_stats[:, :, :quarter].reshape(3, n_req * quarter)
    stats = lax.all_to_all(
        jnp.broadcast_to(local_stats[None], (n_req,) + local_stats.shape),
        "req",
        split_axis=0,
        concat_axis=0,
        tiled=True,
    )
    joint_max = jnp.max(stats[:, 0], axis=0)
    joint_sum = jnp.sum(stats[:, 1] * jnp.exp(stats[:, 0] - joint_max[None]), axis=0)
    joint_pick = jnp.sum(stats[:, 2], axis=0)
    plane_logprob = (joint_pick - joint_max - jnp.log(joint_sum)).reshape(n_req, quarter)
    own_requests = req_id * slots + jnp.arange(slots, dtype=jnp.int32)
    slot_ids = jnp.arange(dealing.shape[0], dtype=jnp.int32)
    serving = jnp.sum(
        jnp.where(dealing[None, :] == own_requests[:, None], slot_ids[None, :], 0), axis=1
    )
    source = serving // slots
    held = (serving % slots) == own_slot
    lp_rows = jnp.take(plane_logprob, source, axis=0)
    node_half = jnp.arange(tree_size, dtype=jnp.int32) // quarter == tp_id % halves
    lp_full = jnp.where(
        held[:, None] & node_half[None, :], jnp.tile(lp_rows, (1, halves)), 0.0
    )
    state_rows = jnp.take(gathered[:, quarter:], source, axis=0).astype(jnp.float32)
    state_rows = jnp.where(held[:, None, None], state_rows, 0.0)
    state_parts = state_rows.reshape(slots * acc_rows, n_tp, dslice).transpose(1, 0, 2)
    outgoing = jnp.concatenate(
        [
            state_parts.reshape(n_tp, slots * acc_rows * dslice),
            jnp.broadcast_to(lp_full.reshape(1, -1), (n_tp, slots * tree_size)),
        ],
        axis=1,
    )
    incoming = lax.all_to_all(outgoing, "tp", split_axis=0, concat_axis=0, tiled=True)
    merged = jnp.sum(incoming, axis=0)
    accepted_state = (
        merged[: slots * acc_rows * dslice].reshape(slots, acc_rows, dslice).astype(jnp.bfloat16)
    )
    target_logprob = merged[slots * acc_rows * dslice :].reshape(slots, tree_size)
    return (target_logprob, accepted_state)


def solution(mesh):
    placed = (
        P("req", None, None),
        P("req", None, "tp"),
        P("req", None, "tp"),
        P("req", None, "tp"),
        P("req", None, "tp"),
        P("req", None, "tp"),
        P("req"),
        P("req", None),
        P("req", None, None),
        P("tp", None),
        P(),
        P("req", None),
        P(),
        P(),
    )
    return jax.shard_map(
        local,
        mesh=mesh,
        in_specs=placed,
        out_specs=(P("req", None), P("req", None, "tp")),
        check_vma=False,
    )
```

```python
import jax
import jax.numpy as jnp
from jax import lax
from jax.sharding import PartitionSpec as P

HD = 224
ACC = 8


EPS = 1e-05
HIGH = lax.Precision.HIGHEST
block_limit = 512


def combined_all(value, axis, join):
    pieces = jax.tree.map(lambda part: lax.all_gather(part, axis), value)
    head = jax.tree.map(lambda part: part[0], pieces)
    tail = jax.tree.map(lambda part: part[1:], pieces)
    subtotal, _ = lax.scan(lambda subtotal, share: (join(subtotal, share), None), head, tail)
    return subtotal


def ancestry(parents):
    node_count = parents.shape[-1]
    node_ids = jnp.arange(node_count, dtype=jnp.int32)
    stride_map = (parents[..., :, None] == node_ids).astype(jnp.float32)
    reached = jnp.broadcast_to(jnp.eye(node_count, dtype=jnp.float32), stride_map.shape) > 0.5
    for doubling in range((ACC - 1).bit_length()):
        further = lax.optimization_barrier(
            jnp.einsum("rtk,rku->rtu", reached.astype(jnp.float32), stride_map, precision=HIGH)
        )
        reached = jnp.logical_or(reached, further > 0.5)
        stride_map = jnp.einsum("rtk,rku->rtu", stride_map, stride_map, precision=HIGH)
    return reached


def combine_stats(earlier, later):
    joint_max = jnp.maximum(earlier[0], later[0])
    joint_sum = earlier[1] * jnp.exp(earlier[0] - joint_max) + later[1] * jnp.exp(
        later[0] - joint_max
    )
    return (joint_max, joint_sum, earlier[2] + later[2])


def vocab_stats(logits, vocab_ids, wanted, along):
    row_max = jnp.max(logits, axis=along)
    row_sum = jnp.sum(jnp.exp(logits - jnp.expand_dims(row_max, along)), axis=along)
    matches = jnp.expand_dims(vocab_ids, 1 - along) == jnp.expand_dims(wanted, along)
    picked = jnp.sum(jnp.where(matches, logits, 0.0), axis=along)
    return (row_max, row_sum, picked)


def local(
    stream,
    queries,
    key_new,
    value_new,
    cache_key,
    cache_value,
    cache_length,
    parents,
    accept,
    out_weight,
    norm_gain,
    head_weight,
    candidate,
    dealing,
):
    slots, tree_size, qwidth = queries.shape
    model_width = stream.shape[2]
    heads_loc = qwidth // HD
    n_tp = lax.axis_size("tp")
    n_req = lax.axis_size("req")
    tp_id = lax.axis_index("tp")
    req_id = lax.axis_index("req")
    score_scale = HD ** (-0.5)
    cache_cap = cache_key.shape[1]
    column_head = jnp.arange(qwidth, dtype=jnp.int32) // HD
    head_mask = column_head[None, :] == jnp.arange(heads_loc, dtype=jnp.int32)[:, None]
    spread_q = jnp.where(
        head_mask[None, :, None, :], queries[:, None, :, :], jnp.zeros((), queries.dtype)
    ).reshape(slots, heads_loc * tree_size, qwidth)
    past_scores = (
        jnp.einsum("rnd,rkd->rnk", spread_q, cache_key, preferred_element_type=jnp.float32)
        * score_scale
    )
    live = jnp.arange(cache_cap, dtype=jnp.int32)[None, :] < cache_length[:, None]
    past_scores = jnp.where(live[:, None, :], past_scores, -jnp.inf)
    visible = ancestry(parents)
    seen = jnp.broadcast_to(
        visible[:, None], (slots, heads_loc, tree_size, tree_size)
    ).reshape(slots, heads_loc * tree_size, tree_size)
    tree_scores = (
        jnp.einsum("rnd,rkd->rnk", spread_q, key_new, preferred_element_type=jnp.float32)
        * score_scale
    )
    tree_scores = jnp.where(seen, tree_scores, -jnp.inf)
    highest = jnp.maximum(jnp.max(past_scores, axis=2), jnp.max(tree_scores, axis=2))
    past_weights = jnp.exp(past_scores - highest[..., None])
    tree_weights = jnp.exp(tree_scores - highest[..., None])
    denominator = jnp.sum(past_weights, axis=2) + jnp.sum(tree_weights, axis=2)
    mixed = jnp.einsum(
        "rnk,rkd->rnd",
        past_weights.astype(jnp.bfloat16),
        cache_value,
        preferred_element_type=jnp.float32,
    ) + jnp.einsum(
        "rnk,rkd->rnd",
        tree_weights.astype(jnp.bfloat16),
        value_new,
        preferred_element_type=jnp.float32,
    )
    mixed = (mixed / denominator[..., None]).reshape(slots, heads_loc, tree_size, qwidth)
    attention = jnp.sum(
        jnp.where(head_mask[None, :, None, :], mixed, 0.0), axis=1
    ).astype(jnp.bfloat16)
    attention_rows = attention.reshape(slots * tree_size, qwidth)
    rows_all = slots * tree_size
    quarter = rows_all // n_tp
    dslice = model_width // n_tp
    halves = tree_size // quarter
    acc_rows = accept.shape[1]
    own_slot = tp_id // halves
    node_off = (tp_id % halves) * quarter
    partial_out = jnp.dot(
        attention_rows, out_weight, preferred_element_type=jnp.float32
    ).astype(jnp.bfloat16)
    arriving = lax.all_to_all(
        partial_out.reshape(n_tp, quarter, model_width), "tp", split_axis=0, concat_axis=0, tiled=True
    )
    summed = jnp.sum(arriving.astype(jnp.float32), axis=0)
    flat_stream = stream.reshape(rows_all, model_width)
    own_stream = lax.dynamic_slice_in_dim(flat_stream, tp_id * quarter, quarter, 0)
    post_rows = (own_stream.astype(jnp.float32) + summed).astype(jnp.bfloat16)
    post_float = post_rows.astype(jnp.float32)
    square = jnp.sum(post_float * post_float, axis=1)
    inverse = lax.rsqrt(square / model_width + EPS)
    normed = (post_float * inverse[:, None] * norm_gain[None, :]).astype(jnp.bfloat16)
    accept_own = lax.dynamic_slice_in_dim(
        lax.dynamic_index_in_dim(accept, own_slot, 0, keepdims=False), node_off, quarter, 1
    )
    picked_rows = jnp.dot(
        accept_own.astype(jnp.bfloat16), post_rows, preferred_element_type=jnp.float32
    ).astype(jnp.bfloat16)
    all_rows = lax.all_gather(normed, "req", axis=0, tiled=True)
    picked_all = lax.all_gather(picked_rows, "req", axis=0, tiled=True).reshape(
        n_req, acc_rows, model_width
    )
    vocab_loc = head_weight.shape[0]
    wanted_rows = lax.dynamic_slice_in_dim(
        candidate.reshape(n_req, rows_all), tp_id * quarter, quarter, 1
    ).reshape(-1)
    vocab_ids = req_id * vocab_loc + jnp.arange(vocab_loc, dtype=jnp.int32)
    logits = lax.dot_general(
        all_rows, head_weight, (((1,), (1,)), ((), ())), preferred_element_type=jnp.float32
    )
    row_max, row_sum, picked = vocab_stats(logits, vocab_ids, wanted_rows, 1)
    local_stats = jnp.stack([row_max, row_sum, picked])
    stats = lax.all_to_all(
        jnp.broadcast_to(local_stats[None], (n_req,) + local_stats.shape),
        "req",
        split_axis=0,
        concat_axis=0,
        tiled=True,
    )
    joint_max = jnp.max(stats[:, 0], axis=0)
    joint_sum = jnp.sum(stats[:, 1] * jnp.exp(stats[:, 0] - joint_max[None]), axis=0)
    joint_pick = jnp.sum(stats[:, 2], axis=0)
    plane_logprob = (joint_pick - joint_max - jnp.log(joint_sum)).reshape(n_req, quarter)
    own_requests = req_id * slots + jnp.arange(slots, dtype=jnp.int32)
    slot_ids = jnp.arange(dealing.shape[0], dtype=jnp.int32)
    serving = jnp.sum(
        jnp.where(dealing[None, :] == own_requests[:, None], slot_ids[None, :], 0), axis=1
    )
    source = serving // slots
    held = (serving % slots) == own_slot
    lp_rows = jnp.take(plane_logprob, source, axis=0)
    node_half = jnp.arange(tree_size, dtype=jnp.int32) // quarter == tp_id % halves
    lp_full = jnp.where(
        held[:, None] & node_half[None, :], jnp.tile(lp_rows, (1, halves)), 0.0
    )
    state_rows = jnp.take(picked_all, source, axis=0).astype(jnp.float32)
    state_rows = jnp.where(held[:, None, None], state_rows, 0.0)
    state_parts = state_rows.reshape(slots * acc_rows, n_tp, dslice).transpose(1, 0, 2)
    outgoing = jnp.concatenate(
        [
            state_parts.reshape(n_tp, slots * acc_rows * dslice),
            jnp.broadcast_to(lp_full.reshape(1, -1), (n_tp, slots * tree_size)),
        ],
        axis=1,
    )
    incoming = lax.all_to_all(outgoing, "tp", split_axis=0, concat_axis=0, tiled=True)
    merged = jnp.sum(incoming, axis=0)
    accepted_state = (
        merged[: slots * acc_rows * dslice].reshape(slots, acc_rows, dslice).astype(jnp.bfloat16)
    )
    target_logprob = merged[slots * acc_rows * dslice :].reshape(slots, tree_size)
    return (target_logprob, accepted_state)


def solution(mesh):
    placed = (
        P("req", None, None),
        P("req", None, "tp"),
        P("req", None, "tp"),
        P("req", None, "tp"),
        P("req", None, "tp"),
        P("req", None, "tp"),
        P("req"),
        P("req", None),
        P("req", None, None),
        P("tp", None),
        P(),
        P("req", None),
        P(),
        P(),
    )
    return jax.shard_map(
        local,
        mesh=mesh,
        in_specs=placed,
        out_specs=(P("req", None), P("req", None, "tp")),
        check_vma=False,
    )
```

```python
import jax
import jax.numpy as jnp
from jax import lax
from jax.sharding import PartitionSpec as P

HD = 224
ACC = 8


EPS = 1e-05
HIGH = lax.Precision.HIGHEST
block_limit = 512


def combined_all(value, axis, join):
    pieces = jax.tree.map(lambda part: lax.all_gather(part, axis), value)
    head = jax.tree.map(lambda part: part[0], pieces)
    tail = jax.tree.map(lambda part: part[1:], pieces)
    subtotal, _ = lax.scan(lambda subtotal, share: (join(subtotal, share), None), head, tail)
    return subtotal


def ancestry(parents):
    node_count = parents.shape[-1]
    node_ids = jnp.arange(node_count, dtype=jnp.int32)
    stride_map = (parents[..., :, None] == node_ids).astype(jnp.float32)
    reached = jnp.broadcast_to(jnp.eye(node_count, dtype=jnp.float32), stride_map.shape) > 0.5
    for doubling in range((ACC - 1).bit_length()):
        further = lax.optimization_barrier(
            jnp.einsum("rtk,rku->rtu", reached.astype(jnp.float32), stride_map, precision=HIGH)
        )
        reached = jnp.logical_or(reached, further > 0.5)
        stride_map = jnp.einsum("rtk,rku->rtu", stride_map, stride_map, precision=HIGH)
    return reached


def combine_stats(earlier, later):
    joint_max = jnp.maximum(earlier[0], later[0])
    joint_sum = earlier[1] * jnp.exp(earlier[0] - joint_max) + later[1] * jnp.exp(
        later[0] - joint_max
    )
    return (joint_max, joint_sum, earlier[2] + later[2])


def vocab_stats(logits, vocab_ids, wanted, along):
    row_max = jnp.max(logits, axis=along)
    row_sum = jnp.sum(jnp.exp(logits - jnp.expand_dims(row_max, along)), axis=along)
    matches = jnp.expand_dims(vocab_ids, 1 - along) == jnp.expand_dims(wanted, along)
    picked = jnp.sum(jnp.where(matches, logits, 0.0), axis=along)
    return (row_max, row_sum, picked)


def local(
    stream,
    queries,
    key_new,
    value_new,
    cache_key,
    cache_value,
    cache_length,
    parents,
    accept,
    out_weight,
    norm_gain,
    head_weight,
    candidate,
    dealing,
):
    slots, tree_size, qwidth = queries.shape
    model_width = stream.shape[2]
    heads_loc = qwidth // HD
    n_tp = lax.axis_size("tp")
    n_req = lax.axis_size("req")
    tp_id = lax.axis_index("tp")
    req_id = lax.axis_index("req")
    score_scale = HD ** (-0.5)
    cache_cap = cache_key.shape[1]
    column_head = jnp.arange(qwidth, dtype=jnp.int32) // HD
    head_mask = column_head[None, :] == jnp.arange(heads_loc, dtype=jnp.int32)[:, None]
    spread_q = jnp.where(
        head_mask[None, :, None, :], queries[:, None, :, :], jnp.zeros((), queries.dtype)
    ).reshape(slots, heads_loc * tree_size, qwidth)
    past_scores = (
        jnp.einsum("rnd,rkd->rnk", spread_q, cache_key, preferred_element_type=jnp.float32)
        * score_scale
    )
    live = jnp.arange(cache_cap, dtype=jnp.int32)[None, :] < cache_length[:, None]
    past_scores = jnp.where(live[:, None, :], past_scores, -jnp.inf)
    visible = ancestry(parents)
    seen = jnp.broadcast_to(
        visible[:, None], (slots, heads_loc, tree_size, tree_size)
    ).reshape(slots, heads_loc * tree_size, tree_size)
    tree_scores = (
        jnp.einsum("rnd,rkd->rnk", spread_q, key_new, preferred_element_type=jnp.float32)
        * score_scale
    )
    tree_scores = jnp.where(seen, tree_scores, -jnp.inf)
    highest = jnp.maximum(jnp.max(past_scores, axis=2), jnp.max(tree_scores, axis=2))
    past_weights = jnp.exp(past_scores - highest[..., None])
    tree_weights = jnp.exp(tree_scores - highest[..., None])
    denominator = jnp.sum(past_weights, axis=2) + jnp.sum(tree_weights, axis=2)
    mixed = jnp.einsum(
        "rnk,rkd->rnd",
        past_weights.astype(jnp.bfloat16),
        cache_value,
        preferred_element_type=jnp.float32,
    ) + jnp.einsum(
        "rnk,rkd->rnd",
        tree_weights.astype(jnp.bfloat16),
        value_new,
        preferred_element_type=jnp.float32,
    )
    mixed = (mixed / denominator[..., None]).reshape(slots, heads_loc, tree_size, qwidth)
    attention = jnp.sum(
        jnp.where(head_mask[None, :, None, :], mixed, 0.0), axis=1
    ).astype(jnp.bfloat16)
    attention_rows = attention.reshape(slots * tree_size, qwidth)
    rows_all = slots * tree_size
    quarter = rows_all // n_tp
    dslice = model_width // n_tp
    halves = tree_size // quarter
    acc_rows = accept.shape[1]
    own_slot = tp_id // halves
    node_off = (tp_id % halves) * quarter
    partial_out = jnp.dot(
        attention_rows, out_weight, preferred_element_type=jnp.float32
    ).astype(jnp.bfloat16)
    arriving = lax.all_to_all(
        partial_out.reshape(n_tp, quarter, model_width), "tp", split_axis=0, concat_axis=0, tiled=True
    )
    summed = jnp.sum(arriving.astype(jnp.float32), axis=0)
    flat_stream = stream.reshape(rows_all, model_width)
    own_stream = lax.dynamic_slice_in_dim(flat_stream, tp_id * quarter, quarter, 0)
    post_rows = (own_stream.astype(jnp.float32) + summed).astype(jnp.bfloat16)
    post_float = post_rows.astype(jnp.float32)
    square = jnp.sum(post_float * post_float, axis=1)
    inverse = lax.rsqrt(square / model_width + EPS)
    normed = (post_float * inverse[:, None] * norm_gain[None, :]).astype(jnp.bfloat16)
    accept_own = lax.dynamic_slice_in_dim(
        lax.dynamic_index_in_dim(accept, own_slot, 0, keepdims=False), node_off, quarter, 1
    )
    picked_rows = jnp.dot(
        accept_own.astype(jnp.bfloat16), post_rows, preferred_element_type=jnp.float32
    ).astype(jnp.bfloat16)
    payload = jnp.concatenate([normed, picked_rows], axis=0)
    gathered = lax.all_gather(payload, "req", axis=0, tiled=True).reshape(
        n_req, quarter + acc_rows, model_width
    )
    all_rows = gathered.reshape(n_req * (quarter + acc_rows), model_width)
    vocab_loc = head_weight.shape[0]
    wanted_rows = jnp.concatenate(
        [
            lax.dynamic_slice_in_dim(
                candidate.reshape(n_req, rows_all), tp_id * quarter, quarter, 1
            ),
            jnp.zeros((n_req, acc_rows), candidate.dtype),
        ],
        axis=1,
    ).reshape(-1)
    vocab_ids = req_id * vocab_loc + jnp.arange(vocab_loc, dtype=jnp.int32)
    logits = lax.dot_general(
        all_rows, head_weight, (((1,), (1,)), ((), ())), preferred_element_type=jnp.float32
    )
    n_slots = dealing.shape[0]
    slot_ids = jnp.arange(n_slots, dtype=jnp.int32)
    serving_all = jnp.sum(
        jnp.where(dealing[None, :] == slot_ids[:, None], slot_ids[None, :], 0), axis=1
    )
    own_serving = lax.dynamic_slice_in_dim(serving_all, req_id * slots, slots, 0)
    held = (own_serving % slots) == own_slot
    state_rows = jnp.take(gathered[:, quarter:], own_serving // slots, axis=0)
    state_rows = jnp.where(held[:, None, None], state_rows, jnp.zeros((), state_rows.dtype))
    state_parts = state_rows.reshape(slots * acc_rows, n_tp, dslice).transpose(1, 0, 2)
    state_in = lax.all_to_all(state_parts, "tp", split_axis=0, concat_axis=0, tiled=True)
    accepted_state = (
        jnp.sum(state_in.astype(jnp.float32), axis=0)
        .reshape(slots, acc_rows, dslice)
        .astype(jnp.bfloat16)
    )
    row_max, row_sum, picked = vocab_stats(logits, vocab_ids, wanted_rows, 1)
    local_stats = jnp.stack([row_max, row_sum, picked]).reshape(3, n_req, quarter + acc_rows)
    local_stats = local_stats[:, :, :quarter].transpose(1, 0, 2)
    dest_blocks = (serving_all // slots).reshape(n_req, 1, slots)
    dest_blocks = jnp.broadcast_to(dest_blocks, (n_req, n_tp, slots)).reshape(-1)
    outgoing = jnp.take(local_stats, dest_blocks, axis=0).reshape(
        n_req * n_tp, slots, 3, quarter
    )
    incoming = lax.all_to_all(
        outgoing, ("req", "tp"), split_axis=0, concat_axis=0, tiled=True
    ).reshape(n_req, n_tp, slots, 3, quarter)
    plane_of = (own_serving % slots)[:, None] * halves + jnp.arange(halves, dtype=jnp.int32)[None, :]
    chosen = jnp.stack(
        [
            jnp.stack(
                [jnp.take(incoming[:, :, i], plane_of[i, h], axis=1) for h in range(halves)],
                axis=1,
            )
            for i in range(slots)
        ],
        axis=1,
    )
    joint_max = jnp.max(chosen[:, :, :, 0], axis=0)
    joint_sum = jnp.sum(chosen[:, :, :, 1] * jnp.exp(chosen[:, :, :, 0] - joint_max[None]), axis=0)
    joint_pick = jnp.sum(chosen[:, :, :, 2], axis=0)
    target_logprob = (joint_pick - joint_max - jnp.log(joint_sum)).reshape(slots, tree_size)
    return (target_logprob, accepted_state)


def solution(mesh):
    placed = (
        P("req", None, None),
        P("req", None, "tp"),
        P("req", None, "tp"),
        P("req", None, "tp"),
        P("req", None, "tp"),
        P("req", None, "tp"),
        P("req"),
        P("req", None),
        P("req", None, None),
        P("tp", None),
        P(),
        P("req", None),
        P(),
        P(),
    )
    return jax.shard_map(
        local,
        mesh=mesh,
        in_specs=placed,
        out_specs=(P("req", None), P("req", None, "tp")),
        check_vma=False,
    )
```

```python
import jax
import jax.numpy as jnp
from jax import lax
from jax.sharding import PartitionSpec as P

HD = 224
ACC = 8


EPS = 1e-05
HIGH = lax.Precision.HIGHEST
block_limit = 512


def combined_all(value, axis, join):
    pieces = jax.tree.map(lambda part: lax.all_gather(part, axis), value)
    head = jax.tree.map(lambda part: part[0], pieces)
    tail = jax.tree.map(lambda part: part[1:], pieces)
    subtotal, _ = lax.scan(lambda subtotal, share: (join(subtotal, share), None), head, tail)
    return subtotal


def ancestry(parents):
    node_count = parents.shape[-1]
    node_ids = jnp.arange(node_count, dtype=jnp.int32)
    stride_map = (parents[..., :, None] == node_ids).astype(jnp.float32)
    reached = jnp.broadcast_to(jnp.eye(node_count, dtype=jnp.float32), stride_map.shape) > 0.5
    for doubling in range((ACC - 1).bit_length()):
        further = lax.optimization_barrier(
            jnp.einsum("rtk,rku->rtu", reached.astype(jnp.float32), stride_map, precision=HIGH)
        )
        reached = jnp.logical_or(reached, further > 0.5)
        stride_map = jnp.einsum("rtk,rku->rtu", stride_map, stride_map, precision=HIGH)
    return reached


def combine_stats(earlier, later):
    joint_max = jnp.maximum(earlier[0], later[0])
    joint_sum = earlier[1] * jnp.exp(earlier[0] - joint_max) + later[1] * jnp.exp(
        later[0] - joint_max
    )
    return (joint_max, joint_sum, earlier[2] + later[2])


def vocab_stats(logits, vocab_ids, wanted, along):
    row_max = jnp.max(logits, axis=along)
    row_sum = jnp.sum(jnp.exp(logits - jnp.expand_dims(row_max, along)), axis=along)
    matches = jnp.expand_dims(vocab_ids, 1 - along) == jnp.expand_dims(wanted, along)
    picked = jnp.sum(jnp.where(matches, logits, 0.0), axis=along)
    return (row_max, row_sum, picked)


def local(
    stream,
    queries,
    key_new,
    value_new,
    cache_key,
    cache_value,
    cache_length,
    parents,
    accept,
    out_weight,
    norm_gain,
    head_weight,
    candidate,
    dealing,
):
    slots, tree_size, qwidth = queries.shape
    model_width = stream.shape[2]
    heads_loc = qwidth // HD
    n_tp = lax.axis_size("tp")
    n_req = lax.axis_size("req")
    tp_id = lax.axis_index("tp")
    req_id = lax.axis_index("req")
    score_scale = HD ** (-0.5)
    cache_cap = cache_key.shape[1]
    column_head = jnp.arange(qwidth, dtype=jnp.int32) // HD
    head_mask = column_head[None, :] == jnp.arange(heads_loc, dtype=jnp.int32)[:, None]
    spread_q = jnp.where(
        head_mask[None, :, None, :], queries[:, None, :, :], jnp.zeros((), queries.dtype)
    ).reshape(slots, heads_loc * tree_size, qwidth)
    past_scores = (
        jnp.einsum("rnd,rkd->rnk", spread_q, cache_key, preferred_element_type=jnp.float32)
        * score_scale
    )
    live = jnp.arange(cache_cap, dtype=jnp.int32)[None, :] < cache_length[:, None]
    past_scores = jnp.where(live[:, None, :], past_scores, -jnp.inf)
    visible = ancestry(parents)
    seen = jnp.broadcast_to(
        visible[:, None], (slots, heads_loc, tree_size, tree_size)
    ).reshape(slots, heads_loc * tree_size, tree_size)
    tree_scores = (
        jnp.einsum("rnd,rkd->rnk", spread_q, key_new, preferred_element_type=jnp.float32)
        * score_scale
    )
    tree_scores = jnp.where(seen, tree_scores, -jnp.inf)
    highest = jnp.maximum(jnp.max(past_scores, axis=2), jnp.max(tree_scores, axis=2))
    past_weights = jnp.exp(past_scores - highest[..., None])
    tree_weights = jnp.exp(tree_scores - highest[..., None])
    denominator = jnp.sum(past_weights, axis=2) + jnp.sum(tree_weights, axis=2)
    mixed = jnp.einsum(
        "rnk,rkd->rnd",
        past_weights.astype(jnp.bfloat16),
        cache_value,
        preferred_element_type=jnp.float32,
    ) + jnp.einsum(
        "rnk,rkd->rnd",
        tree_weights.astype(jnp.bfloat16),
        value_new,
        preferred_element_type=jnp.float32,
    )
    mixed = (mixed / denominator[..., None]).reshape(slots, heads_loc, tree_size, qwidth)
    attention = jnp.sum(
        jnp.where(head_mask[None, :, None, :], mixed, 0.0), axis=1
    ).astype(jnp.bfloat16)
    attention_rows = attention.reshape(slots * tree_size, qwidth)
    rows_all = slots * tree_size
    quarter = rows_all // n_tp
    dslice = model_width // n_tp
    halves = tree_size // quarter
    acc_rows = accept.shape[1]
    own_slot = tp_id // halves
    node_off = (tp_id % halves) * quarter
    partial_out = jnp.dot(
        attention_rows, out_weight, preferred_element_type=jnp.float32
    ).astype(jnp.bfloat16)
    arriving = lax.all_to_all(
        partial_out.reshape(n_tp, quarter, model_width), "tp", split_axis=0, concat_axis=0, tiled=True
    )
    summed = jnp.sum(arriving.astype(jnp.float32), axis=0)
    flat_stream = stream.reshape(rows_all, model_width)
    own_stream = lax.dynamic_slice_in_dim(flat_stream, tp_id * quarter, quarter, 0)
    post_rows = (own_stream.astype(jnp.float32) + summed).astype(jnp.bfloat16)
    post_float = post_rows.astype(jnp.float32)
    square = jnp.sum(post_float * post_float, axis=1)
    inverse = lax.rsqrt(square / model_width + EPS)
    normed = (post_float * inverse[:, None] * norm_gain[None, :]).astype(jnp.bfloat16)
    accept_own = lax.dynamic_slice_in_dim(
        lax.dynamic_index_in_dim(accept, own_slot, 0, keepdims=False), node_off, quarter, 1
    )
    picked_rows = jnp.dot(
        accept_own.astype(jnp.bfloat16), post_rows, preferred_element_type=jnp.float32
    ).astype(jnp.bfloat16)
    n_slots = dealing.shape[0]
    global_slot = req_id * slots + own_slot
    owner = lax.dynamic_index_in_dim(dealing, global_slot, 0, keepdims=False) // slots
    dest_req = jnp.arange(n_req * n_tp, dtype=jnp.int32) // n_tp
    picked_parts = picked_rows.reshape(acc_rows, n_tp, dslice).transpose(1, 0, 2)
    picked_out = jnp.where(
        (dest_req == owner)[:, None, None],
        jnp.tile(picked_parts, (n_req, 1, 1)),
        jnp.zeros((), picked_parts.dtype),
    )
    picked_in = lax.all_to_all(
        picked_out, ("req", "tp"), split_axis=0, concat_axis=0, tiled=True
    )
    all_rows = lax.all_gather(normed, "req", axis=0, tiled=True)
    vocab_loc = head_weight.shape[0]
    wanted_rows = lax.dynamic_slice_in_dim(
        candidate.reshape(n_req, rows_all), tp_id * quarter, quarter, 1
    ).reshape(-1)
    vocab_ids = req_id * vocab_loc + jnp.arange(vocab_loc, dtype=jnp.int32)
    logits = lax.dot_general(
        all_rows, head_weight, (((1,), (1,)), ((), ())), preferred_element_type=jnp.float32
    )
    slot_ids = jnp.arange(n_slots, dtype=jnp.int32)
    serving_all = jnp.sum(
        jnp.where(dealing[None, :] == slot_ids[:, None], slot_ids[None, :], 0), axis=1
    )
    own_serving = lax.dynamic_slice_in_dim(serving_all, req_id * slots, slots, 0)
    source_slot = (
        jnp.arange(n_req * n_tp, dtype=jnp.int32) // n_tp * slots
        + jnp.arange(n_req * n_tp, dtype=jnp.int32) % n_tp // halves
    )
    source_request = jnp.take(dealing, source_slot)
    routed = (source_request[None, :] == (req_id * slots + jnp.arange(slots, dtype=jnp.int32))[:, None])
    accepted_state = jnp.einsum(
        "ks,sad->kad",
        routed.astype(jnp.bfloat16),
        picked_in,
        preferred_element_type=jnp.float32,
    ).astype(jnp.bfloat16)
    row_max, row_sum, picked = vocab_stats(logits, vocab_ids, wanted_rows, 1)
    local_stats = jnp.stack([row_max, row_sum, picked]).reshape(3, n_req, quarter)
    local_stats = local_stats.transpose(1, 0, 2)
    dest_blocks = (serving_all // slots).reshape(n_req, 1, slots)
    dest_blocks = jnp.broadcast_to(dest_blocks, (n_req, n_tp, slots)).reshape(-1)
    outgoing = jnp.take(local_stats, dest_blocks, axis=0).reshape(
        n_req * n_tp, slots, 3, quarter
    )
    incoming = lax.all_to_all(
        outgoing, ("req", "tp"), split_axis=0, concat_axis=0, tiled=True
    ).reshape(n_req, n_tp, slots, 3, quarter)
    plane_of = (own_serving % slots)[:, None] * halves + jnp.arange(halves, dtype=jnp.int32)[None, :]
    chosen = jnp.stack(
        [
            jnp.stack(
                [jnp.take(incoming[:, :, i], plane_of[i, h], axis=1) for h in range(halves)],
                axis=1,
            )
            for i in range(slots)
        ],
        axis=1,
    )
    joint_max = jnp.max(chosen[:, :, :, 0], axis=0)
    joint_sum = jnp.sum(chosen[:, :, :, 1] * jnp.exp(chosen[:, :, :, 0] - joint_max[None]), axis=0)
    joint_pick = jnp.sum(chosen[:, :, :, 2], axis=0)
    target_logprob = (joint_pick - joint_max - jnp.log(joint_sum)).reshape(slots, tree_size)
    return (target_logprob, accepted_state)


def solution(mesh):
    placed = (
        P("req", None, None),
        P("req", None, "tp"),
        P("req", None, "tp"),
        P("req", None, "tp"),
        P("req", None, "tp"),
        P("req", None, "tp"),
        P("req"),
        P("req", None),
        P("req", None, None),
        P("tp", None),
        P(),
        P("req", None),
        P(),
        P(),
    )
    return jax.shard_map(
        local,
        mesh=mesh,
        in_specs=placed,
        out_specs=(P("req", None), P("req", None, "tp")),
        check_vma=False,
    )
```

```python
import jax
import jax.numpy as jnp
from jax import lax
from jax.sharding import PartitionSpec as P

HD = 224
ACC = 8


EPS = 1e-05
HIGH = lax.Precision.HIGHEST
block_limit = 512


def combined_all(value, axis, join):
    pieces = jax.tree.map(lambda part: lax.all_gather(part, axis), value)
    head = jax.tree.map(lambda part: part[0], pieces)
    tail = jax.tree.map(lambda part: part[1:], pieces)
    subtotal, _ = lax.scan(lambda subtotal, share: (join(subtotal, share), None), head, tail)
    return subtotal


def ancestry(parents):
    node_count = parents.shape[-1]
    node_ids = jnp.arange(node_count, dtype=jnp.int32)
    stride_map = (parents[..., :, None] == node_ids).astype(jnp.float32)
    reached = jnp.broadcast_to(jnp.eye(node_count, dtype=jnp.float32), stride_map.shape) > 0.5
    for doubling in range((ACC - 1).bit_length()):
        further = lax.optimization_barrier(
            jnp.einsum("rtk,rku->rtu", reached.astype(jnp.float32), stride_map, precision=HIGH)
        )
        reached = jnp.logical_or(reached, further > 0.5)
        stride_map = jnp.einsum("rtk,rku->rtu", stride_map, stride_map, precision=HIGH)
    return reached


def combine_stats(earlier, later):
    joint_max = jnp.maximum(earlier[0], later[0])
    joint_sum = earlier[1] * jnp.exp(earlier[0] - joint_max) + later[1] * jnp.exp(
        later[0] - joint_max
    )
    return (joint_max, joint_sum, earlier[2] + later[2])


def vocab_stats(logits, vocab_ids, wanted, along):
    row_max = jnp.max(logits, axis=along)
    row_sum = jnp.sum(jnp.exp(logits - jnp.expand_dims(row_max, along)), axis=along)
    matches = jnp.expand_dims(vocab_ids, 1 - along) == jnp.expand_dims(wanted, along)
    picked = jnp.sum(jnp.where(matches, logits, 0.0), axis=along)
    return (row_max, row_sum, picked)


def local(
    stream,
    queries,
    key_new,
    value_new,
    cache_key,
    cache_value,
    cache_length,
    parents,
    accept,
    out_weight,
    norm_gain,
    head_weight,
    candidate,
    dealing,
):
    slots, tree_size, qwidth = queries.shape
    model_width = stream.shape[2]
    heads_loc = qwidth // HD
    n_tp = lax.axis_size("tp")
    n_req = lax.axis_size("req")
    tp_id = lax.axis_index("tp")
    req_id = lax.axis_index("req")
    score_scale = HD ** (-0.5)
    cache_cap = cache_key.shape[1]
    column_head = jnp.arange(qwidth, dtype=jnp.int32) // HD
    head_mask = column_head[None, :] == jnp.arange(heads_loc, dtype=jnp.int32)[:, None]
    spread_q = jnp.where(
        head_mask[None, :, None, :], queries[:, None, :, :], jnp.zeros((), queries.dtype)
    ).reshape(slots, heads_loc * tree_size, qwidth)
    past_scores = (
        jnp.einsum("rnd,rkd->rnk", spread_q, cache_key, preferred_element_type=jnp.float32)
        * score_scale
    )
    live = jnp.arange(cache_cap, dtype=jnp.int32)[None, :] < cache_length[:, None]
    past_scores = jnp.where(live[:, None, :], past_scores, -jnp.inf)
    visible = ancestry(parents)
    seen = jnp.broadcast_to(
        visible[:, None], (slots, heads_loc, tree_size, tree_size)
    ).reshape(slots, heads_loc * tree_size, tree_size)
    tree_scores = (
        jnp.einsum("rnd,rkd->rnk", spread_q, key_new, preferred_element_type=jnp.float32)
        * score_scale
    )
    tree_scores = jnp.where(seen, tree_scores, -jnp.inf)
    highest = jnp.maximum(jnp.max(past_scores, axis=2), jnp.max(tree_scores, axis=2))
    past_weights = jnp.exp(past_scores - highest[..., None])
    tree_weights = jnp.exp(tree_scores - highest[..., None])
    denominator = jnp.sum(past_weights, axis=2) + jnp.sum(tree_weights, axis=2)
    mixed = jnp.einsum(
        "rnk,rkd->rnd",
        past_weights.astype(jnp.bfloat16),
        cache_value,
        preferred_element_type=jnp.float32,
    ) + jnp.einsum(
        "rnk,rkd->rnd",
        tree_weights.astype(jnp.bfloat16),
        value_new,
        preferred_element_type=jnp.float32,
    )
    mixed = (mixed / denominator[..., None]).reshape(slots, heads_loc, tree_size, qwidth)
    attention = jnp.sum(
        jnp.where(head_mask[None, :, None, :], mixed, 0.0), axis=1
    ).astype(jnp.bfloat16)
    attention_rows = attention.reshape(slots * tree_size, qwidth)
    rows_all = slots * tree_size
    quarter = rows_all // n_tp
    dslice = model_width // n_tp
    halves = tree_size // quarter
    acc_rows = accept.shape[1]
    own_slot = tp_id // halves
    node_off = (tp_id % halves) * quarter
    partial_out = jnp.dot(
        attention_rows, out_weight, preferred_element_type=jnp.float32
    ).astype(jnp.bfloat16)
    arriving = lax.all_to_all(
        partial_out.reshape(n_tp, quarter, model_width), "tp", split_axis=0, concat_axis=0, tiled=True
    )
    summed = jnp.sum(arriving.astype(jnp.float32), axis=0)
    flat_stream = stream.reshape(rows_all, model_width)
    own_stream = lax.dynamic_slice_in_dim(flat_stream, tp_id * quarter, quarter, 0)
    post_rows = (own_stream.astype(jnp.float32) + summed).astype(jnp.bfloat16)
    post_float = post_rows.astype(jnp.float32)
    square = jnp.sum(post_float * post_float, axis=1)
    inverse = lax.rsqrt(square / model_width + EPS)
    normed = (post_float * inverse[:, None] * norm_gain[None, :]).astype(jnp.bfloat16)
    accept_own = lax.dynamic_slice_in_dim(
        lax.dynamic_index_in_dim(accept, own_slot, 0, keepdims=False), node_off, quarter, 1
    )
    picked_rows = jnp.dot(
        accept_own.astype(jnp.bfloat16), post_rows, preferred_element_type=jnp.float32
    ).astype(jnp.bfloat16)
    n_slots = dealing.shape[0]
    global_slot = req_id * slots + own_slot
    slot_ids = jnp.arange(n_slots, dtype=jnp.int32)
    owner = jnp.sum(jnp.where(slot_ids == global_slot, dealing, 0)) // slots
    dest_req = jnp.arange(n_req * n_tp, dtype=jnp.int32) // n_tp
    picked_parts = picked_rows.reshape(acc_rows, n_tp, dslice).transpose(1, 0, 2)
    picked_out = jnp.where(
        (dest_req == owner)[:, None, None],
        jnp.tile(picked_parts, (n_req, 1, 1)),
        jnp.zeros((), picked_parts.dtype),
    )
    picked_in = lax.all_to_all(
        picked_out, ("req", "tp"), split_axis=0, concat_axis=0, tiled=True
    )
    all_rows = lax.all_gather(normed, "req", axis=0, tiled=True)
    vocab_loc = head_weight.shape[0]
    wanted_rows = lax.dynamic_slice_in_dim(
        candidate.reshape(n_req, rows_all), tp_id * quarter, quarter, 1
    ).reshape(-1)
    vocab_ids = req_id * vocab_loc + jnp.arange(vocab_loc, dtype=jnp.int32)
    logits = lax.dot_general(
        all_rows, head_weight, (((1,), (1,)), ((), ())), preferred_element_type=jnp.float32
    )
    serving_all = jnp.sum(
        jnp.where(dealing[None, :] == slot_ids[:, None], slot_ids[None, :], 0), axis=1
    )
    own_requests = req_id * slots + jnp.arange(slots, dtype=jnp.int32)
    own_serving = jnp.sum(
        jnp.where(dealing[None, :] == own_requests[:, None], slot_ids[None, :], 0), axis=1
    )
    source_slot = (
        jnp.arange(n_req * n_tp, dtype=jnp.int32) // n_tp * slots
        + jnp.arange(n_req * n_tp, dtype=jnp.int32) % n_tp // halves
    )
    source_request = jnp.sum(
        jnp.where(source_slot[:, None] == slot_ids[None, :], dealing[None, :], 0), axis=1
    )
    routed = source_request[None, :] == own_requests[:, None]
    accepted_state = jnp.einsum(
        "ks,sad->kad",
        routed.astype(jnp.bfloat16),
        picked_in,
        preferred_element_type=jnp.float32,
    ).astype(jnp.bfloat16)
    row_max, row_sum, picked = vocab_stats(logits, vocab_ids, wanted_rows, 1)
    local_stats = jnp.stack([row_max, row_sum, picked]).reshape(3, n_req, quarter)
    local_stats = local_stats.transpose(1, 0, 2)
    dest_blocks = (serving_all // slots).reshape(n_req, 1, slots)
    dest_blocks = jnp.broadcast_to(dest_blocks, (n_req, n_tp, slots)).reshape(-1)
    block_ids = jnp.arange(n_req, dtype=jnp.int32)
    outgoing = jnp.sum(
        jnp.where(
            (dest_blocks[:, None] == block_ids[None, :])[:, :, None, None],
            local_stats[None],
            0.0,
        ),
        axis=1,
    ).reshape(n_req * n_tp, slots, 3, quarter)
    incoming = lax.all_to_all(
        outgoing, ("req", "tp"), split_axis=0, concat_axis=0, tiled=True
    ).reshape(n_req, n_tp, slots, 3, quarter)
    plane_of = (own_serving % slots)[:, None] * halves + jnp.arange(halves, dtype=jnp.int32)[None, :]
    plane_ids = jnp.arange(n_tp, dtype=jnp.int32)
    chosen = jnp.sum(
        jnp.where(
            (plane_of[:, :, None] == plane_ids[None, None, :])[None, :, :, :, None, None],
            incoming.transpose(0, 2, 1, 3, 4)[:, :, None],
            0.0,
        ),
        axis=3,
    )
    joint_max = jnp.max(chosen[:, :, :, 0], axis=0)
    joint_sum = jnp.sum(chosen[:, :, :, 1] * jnp.exp(chosen[:, :, :, 0] - joint_max[None]), axis=0)
    joint_pick = jnp.sum(chosen[:, :, :, 2], axis=0)
    target_logprob = (joint_pick - joint_max - jnp.log(joint_sum)).reshape(slots, tree_size)
    return (target_logprob, accepted_state)


def solution(mesh):
    placed = (
        P("req", None, None),
        P("req", None, "tp"),
        P("req", None, "tp"),
        P("req", None, "tp"),
        P("req", None, "tp"),
        P("req", None, "tp"),
        P("req"),
        P("req", None),
        P("req", None, None),
        P("tp", None),
        P(),
        P("req", None),
        P(),
        P(),
    )
    return jax.shard_map(
        local,
        mesh=mesh,
        in_specs=placed,
        out_specs=(P("req", None), P("req", None, "tp")),
        check_vma=False,
    )
```

```python
import jax
import jax.numpy as jnp
from jax import lax
from jax.sharding import PartitionSpec as P

HD = 224
ACC = 8


EPS = 1e-05
HIGH = lax.Precision.HIGHEST
block_limit = 512


def combined_all(value, axis, join):
    pieces = jax.tree.map(lambda part: lax.all_gather(part, axis), value)
    head = jax.tree.map(lambda part: part[0], pieces)
    tail = jax.tree.map(lambda part: part[1:], pieces)
    subtotal, _ = lax.scan(lambda subtotal, share: (join(subtotal, share), None), head, tail)
    return subtotal


def ancestry(parents):
    node_count = parents.shape[-1]
    node_ids = jnp.arange(node_count, dtype=jnp.int32)
    stride_map = (parents[..., :, None] == node_ids).astype(jnp.float32)
    reached = jnp.broadcast_to(jnp.eye(node_count, dtype=jnp.float32), stride_map.shape) > 0.5
    for doubling in range((ACC - 1).bit_length()):
        further = lax.optimization_barrier(
            jnp.einsum("rtk,rku->rtu", reached.astype(jnp.float32), stride_map, precision=HIGH)
        )
        reached = jnp.logical_or(reached, further > 0.5)
        stride_map = jnp.einsum("rtk,rku->rtu", stride_map, stride_map, precision=HIGH)
    return reached


def combine_stats(earlier, later):
    joint_max = jnp.maximum(earlier[0], later[0])
    joint_sum = earlier[1] * jnp.exp(earlier[0] - joint_max) + later[1] * jnp.exp(
        later[0] - joint_max
    )
    return (joint_max, joint_sum, earlier[2] + later[2])


def vocab_stats(logits, vocab_ids, wanted, along):
    row_max = jnp.max(logits, axis=along)
    row_sum = jnp.sum(jnp.exp(logits - jnp.expand_dims(row_max, along)), axis=along)
    matches = jnp.expand_dims(vocab_ids, 1 - along) == jnp.expand_dims(wanted, along)
    picked = jnp.sum(jnp.where(matches, logits, 0.0), axis=along)
    return (row_max, row_sum, picked)


def local(
    stream,
    queries,
    key_new,
    value_new,
    cache_key,
    cache_value,
    cache_length,
    parents,
    accept,
    out_weight,
    norm_gain,
    head_weight,
    candidate,
    dealing,
):
    slots, tree_size, qwidth = queries.shape
    model_width = stream.shape[2]
    heads_loc = qwidth // HD
    n_tp = lax.axis_size("tp")
    n_req = lax.axis_size("req")
    tp_id = lax.axis_index("tp")
    req_id = lax.axis_index("req")
    score_scale = HD ** (-0.5)
    cache_cap = cache_key.shape[1]
    column_head = jnp.arange(qwidth, dtype=jnp.int32) // HD
    head_mask = column_head[None, :] == jnp.arange(heads_loc, dtype=jnp.int32)[:, None]
    spread_q = jnp.where(
        head_mask[None, :, None, :], queries[:, None, :, :], jnp.zeros((), queries.dtype)
    ).reshape(slots, heads_loc * tree_size, qwidth)
    past_scores = (
        jnp.einsum("rnd,rkd->rnk", spread_q, cache_key, preferred_element_type=jnp.float32)
        * score_scale
    )
    live = jnp.arange(cache_cap, dtype=jnp.int32)[None, :] < cache_length[:, None]
    past_scores = jnp.where(live[:, None, :], past_scores, -jnp.inf)
    visible = ancestry(parents)
    seen = jnp.broadcast_to(
        visible[:, None], (slots, heads_loc, tree_size, tree_size)
    ).reshape(slots, heads_loc * tree_size, tree_size)
    tree_scores = (
        jnp.einsum("rnd,rkd->rnk", spread_q, key_new, preferred_element_type=jnp.float32)
        * score_scale
    )
    tree_scores = jnp.where(seen, tree_scores, -jnp.inf)
    highest = jnp.maximum(jnp.max(past_scores, axis=2), jnp.max(tree_scores, axis=2))
    past_weights = jnp.exp(past_scores - highest[..., None])
    tree_weights = jnp.exp(tree_scores - highest[..., None])
    denominator = jnp.sum(past_weights, axis=2) + jnp.sum(tree_weights, axis=2)
    mixed = jnp.einsum(
        "rnk,rkd->rnd",
        past_weights.astype(jnp.bfloat16),
        cache_value,
        preferred_element_type=jnp.float32,
    ) + jnp.einsum(
        "rnk,rkd->rnd",
        tree_weights.astype(jnp.bfloat16),
        value_new,
        preferred_element_type=jnp.float32,
    )
    mixed = (mixed / denominator[..., None]).reshape(slots, heads_loc, tree_size, qwidth)
    attention = jnp.sum(
        jnp.where(head_mask[None, :, None, :], mixed, 0.0), axis=1
    ).astype(jnp.bfloat16)
    attention_rows = attention.reshape(slots * tree_size, qwidth)
    rows_all = slots * tree_size
    quarter = rows_all // n_tp
    dslice = model_width // n_tp
    halves = tree_size // quarter
    acc_rows = accept.shape[1]
    own_slot = tp_id // halves
    node_off = (tp_id % halves) * quarter
    partial_out = jnp.dot(
        attention_rows, out_weight, preferred_element_type=jnp.float32
    ).astype(jnp.bfloat16)
    blocks = partial_out.reshape(n_tp, quarter, model_width)
    summed = lax.dynamic_index_in_dim(blocks, tp_id, 0, keepdims=False).astype(jnp.float32)
    for shift in range(1, n_tp):
        outbound = lax.dynamic_index_in_dim(blocks, (tp_id + shift) % n_tp, 0, keepdims=False)
        summed = summed + lax.ppermute(
            outbound, "tp", [(t, (t + shift) % n_tp) for t in range(n_tp)]
        ).astype(jnp.float32)
    flat_stream = stream.reshape(rows_all, model_width)
    own_stream = lax.dynamic_slice_in_dim(flat_stream, tp_id * quarter, quarter, 0)
    post_rows = (own_stream.astype(jnp.float32) + summed).astype(jnp.bfloat16)
    post_float = post_rows.astype(jnp.float32)
    square = jnp.sum(post_float * post_float, axis=1)
    inverse = lax.rsqrt(square / model_width + EPS)
    normed = (post_float * inverse[:, None] * norm_gain[None, :]).astype(jnp.bfloat16)
    accept_own = lax.dynamic_slice_in_dim(
        lax.dynamic_index_in_dim(accept, own_slot, 0, keepdims=False), node_off, quarter, 1
    )
    picked_rows = jnp.dot(
        accept_own.astype(jnp.bfloat16), post_rows, preferred_element_type=jnp.float32
    ).astype(jnp.bfloat16)
    n_slots = dealing.shape[0]
    global_slot = req_id * slots + own_slot
    slot_ids = jnp.arange(n_slots, dtype=jnp.int32)
    owner = jnp.sum(jnp.where(slot_ids == global_slot, dealing, 0)) // slots
    dest_req = jnp.arange(n_req * n_tp, dtype=jnp.int32) // n_tp
    picked_parts = picked_rows.reshape(acc_rows, n_tp, dslice).transpose(1, 0, 2)
    picked_out = jnp.where(
        (dest_req == owner)[:, None, None],
        jnp.tile(picked_parts, (n_req, 1, 1)),
        jnp.zeros((), picked_parts.dtype),
    )
    picked_in = lax.all_to_all(
        picked_out, ("req", "tp"), split_axis=0, concat_axis=0, tiled=True
    )
    all_rows = lax.all_gather(normed, "req", axis=0, tiled=True)
    vocab_loc = head_weight.shape[0]
    wanted_rows = lax.dynamic_slice_in_dim(
        candidate.reshape(n_req, rows_all), tp_id * quarter, quarter, 1
    ).reshape(-1)
    vocab_ids = req_id * vocab_loc + jnp.arange(vocab_loc, dtype=jnp.int32)
    logits = lax.dot_general(
        all_rows, head_weight, (((1,), (1,)), ((), ())), preferred_element_type=jnp.float32
    )
    serving_all = jnp.sum(
        jnp.where(dealing[None, :] == slot_ids[:, None], slot_ids[None, :], 0), axis=1
    )
    own_requests = req_id * slots + jnp.arange(slots, dtype=jnp.int32)
    own_serving = jnp.sum(
        jnp.where(dealing[None, :] == own_requests[:, None], slot_ids[None, :], 0), axis=1
    )
    source_slot = (
        jnp.arange(n_req * n_tp, dtype=jnp.int32) // n_tp * slots
        + jnp.arange(n_req * n_tp, dtype=jnp.int32) % n_tp // halves
    )
    source_request = jnp.sum(
        jnp.where(source_slot[:, None] == slot_ids[None, :], dealing[None, :], 0), axis=1
    )
    routed = source_request[None, :] == own_requests[:, None]
    accepted_state = jnp.einsum(
        "ks,sad->kad",
        routed.astype(jnp.bfloat16),
        picked_in,
        preferred_element_type=jnp.float32,
    ).astype(jnp.bfloat16)
    row_max, row_sum, picked = vocab_stats(logits, vocab_ids, wanted_rows, 1)
    local_stats = jnp.stack([row_max, row_sum, picked]).reshape(3, n_req, quarter)
    local_stats = local_stats.transpose(1, 0, 2)
    dest_blocks = (serving_all // slots).reshape(n_req, 1, slots)
    dest_blocks = jnp.broadcast_to(dest_blocks, (n_req, n_tp, slots)).reshape(-1)
    block_ids = jnp.arange(n_req, dtype=jnp.int32)
    outgoing = jnp.sum(
        jnp.where(
            (dest_blocks[:, None] == block_ids[None, :])[:, :, None, None],
            local_stats[None],
            0.0,
        ),
        axis=1,
    ).reshape(n_req * n_tp, slots, 3, quarter)
    incoming = lax.all_to_all(
        outgoing, ("req", "tp"), split_axis=0, concat_axis=0, tiled=True
    ).reshape(n_req, n_tp, slots, 3, quarter)
    plane_of = (own_serving % slots)[:, None] * halves + jnp.arange(halves, dtype=jnp.int32)[None, :]
    plane_ids = jnp.arange(n_tp, dtype=jnp.int32)
    chosen = jnp.sum(
        jnp.where(
            (plane_of[:, :, None] == plane_ids[None, None, :])[None, :, :, :, None, None],
            incoming.transpose(0, 2, 1, 3, 4)[:, :, None],
            0.0,
        ),
        axis=3,
    )
    joint_max = jnp.max(chosen[:, :, :, 0], axis=0)
    joint_sum = jnp.sum(chosen[:, :, :, 1] * jnp.exp(chosen[:, :, :, 0] - joint_max[None]), axis=0)
    joint_pick = jnp.sum(chosen[:, :, :, 2], axis=0)
    target_logprob = (joint_pick - joint_max - jnp.log(joint_sum)).reshape(slots, tree_size)
    return (target_logprob, accepted_state)


def solution(mesh):
    placed = (
        P("req", None, None),
        P("req", None, "tp"),
        P("req", None, "tp"),
        P("req", None, "tp"),
        P("req", None, "tp"),
        P("req", None, "tp"),
        P("req"),
        P("req", None),
        P("req", None, None),
        P("tp", None),
        P(),
        P("req", None),
        P(),
        P(),
    )
    return jax.shard_map(
        local,
        mesh=mesh,
        in_specs=placed,
        out_specs=(P("req", None), P("req", None, "tp")),
        check_vma=False,
    )
```

```python
import jax
import jax.numpy as jnp
from jax import lax
from jax.sharding import Mesh, PartitionSpec as P

HD = 224
ACC = 8


EPS = 1e-05
HIGH = lax.Precision.HIGHEST
block_limit = 512


def combined_all(value, axis, join):
    pieces = jax.tree.map(lambda part: lax.all_gather(part, axis), value)
    head = jax.tree.map(lambda part: part[0], pieces)
    tail = jax.tree.map(lambda part: part[1:], pieces)
    subtotal, _ = lax.scan(lambda subtotal, share: (join(subtotal, share), None), head, tail)
    return subtotal


def ancestry(parents):
    node_count = parents.shape[-1]
    node_ids = jnp.arange(node_count, dtype=jnp.int32)
    stride_map = (parents[..., :, None] == node_ids).astype(jnp.float32)
    reached = jnp.broadcast_to(jnp.eye(node_count, dtype=jnp.float32), stride_map.shape) > 0.5
    for doubling in range((ACC - 1).bit_length()):
        further = lax.optimization_barrier(
            jnp.einsum("rtk,rku->rtu", reached.astype(jnp.float32), stride_map, precision=HIGH)
        )
        reached = jnp.logical_or(reached, further > 0.5)
        stride_map = jnp.einsum("rtk,rku->rtu", stride_map, stride_map, precision=HIGH)
    return reached


def combine_stats(earlier, later):
    joint_max = jnp.maximum(earlier[0], later[0])
    joint_sum = earlier[1] * jnp.exp(earlier[0] - joint_max) + later[1] * jnp.exp(
        later[0] - joint_max
    )
    return (joint_max, joint_sum, earlier[2] + later[2])


def vocab_stats(logits, vocab_ids, wanted, along):
    row_max = jnp.max(logits, axis=along)
    row_sum = jnp.sum(jnp.exp(logits - jnp.expand_dims(row_max, along)), axis=along)
    matches = jnp.expand_dims(vocab_ids, 1 - along) == jnp.expand_dims(wanted, along)
    picked = jnp.sum(jnp.where(matches, logits, 0.0), axis=along)
    return (row_max, row_sum, picked)


def local(
    stream,
    queries,
    key_new,
    value_new,
    cache_key,
    cache_value,
    cache_length,
    parents,
    accept,
    out_weight,
    norm_gain,
    head_weight,
    candidate,
    dealing,
):
    slots, tree_size, qwidth = queries.shape
    model_width = stream.shape[2]
    heads_loc = qwidth // HD
    n_tp = lax.axis_size("tp")
    n_chip = lax.axis_size("chip")
    n_core = lax.axis_size("core")
    n_req = n_chip * n_core
    tp_id = lax.axis_index("tp")
    chip_id = lax.axis_index("chip")
    core_id = lax.axis_index("core")
    req_id = chip_id * n_core + core_id
    score_scale = HD ** (-0.5)
    cache_cap = cache_key.shape[1]
    column_head = jnp.arange(qwidth, dtype=jnp.int32) // HD
    head_mask = column_head[None, :] == jnp.arange(heads_loc, dtype=jnp.int32)[:, None]
    spread_q = jnp.where(
        head_mask[None, :, None, :], queries[:, None, :, :], jnp.zeros((), queries.dtype)
    ).reshape(slots, heads_loc * tree_size, qwidth)
    past_scores = (
        jnp.einsum("rnd,rkd->rnk", spread_q, cache_key, preferred_element_type=jnp.float32)
        * score_scale
    )
    live = jnp.arange(cache_cap, dtype=jnp.int32)[None, :] < cache_length[:, None]
    past_scores = jnp.where(live[:, None, :], past_scores, -jnp.inf)
    visible = ancestry(parents)
    seen = jnp.broadcast_to(
        visible[:, None], (slots, heads_loc, tree_size, tree_size)
    ).reshape(slots, heads_loc * tree_size, tree_size)
    tree_scores = (
        jnp.einsum("rnd,rkd->rnk", spread_q, key_new, preferred_element_type=jnp.float32)
        * score_scale
    )
    tree_scores = jnp.where(seen, tree_scores, -jnp.inf)
    highest = jnp.maximum(jnp.max(past_scores, axis=2), jnp.max(tree_scores, axis=2))
    past_weights = jnp.exp(past_scores - highest[..., None])
    tree_weights = jnp.exp(tree_scores - highest[..., None])
    denominator = jnp.sum(past_weights, axis=2) + jnp.sum(tree_weights, axis=2)
    mixed = jnp.einsum(
        "rnk,rkd->rnd",
        past_weights.astype(jnp.bfloat16),
        cache_value,
        preferred_element_type=jnp.float32,
    ) + jnp.einsum(
        "rnk,rkd->rnd",
        tree_weights.astype(jnp.bfloat16),
        value_new,
        preferred_element_type=jnp.float32,
    )
    mixed = (mixed / denominator[..., None]).reshape(slots, heads_loc, tree_size, qwidth)
    attention = jnp.sum(
        jnp.where(head_mask[None, :, None, :], mixed, 0.0), axis=1
    ).astype(jnp.bfloat16)
    attention_rows = attention.reshape(slots * tree_size, qwidth)
    rows_all = slots * tree_size
    quarter = rows_all // n_tp
    dslice = model_width // n_tp
    halves = tree_size // quarter
    acc_rows = accept.shape[1]
    own_slot = tp_id // halves
    node_off = (tp_id % halves) * quarter
    partial_out = jnp.dot(
        attention_rows, out_weight, preferred_element_type=jnp.float32
    ).astype(jnp.bfloat16)
    blocks = partial_out.reshape(n_tp, quarter, model_width)
    summed = lax.dynamic_index_in_dim(blocks, tp_id, 0, keepdims=False).astype(jnp.float32)
    for shift in range(1, n_tp):
        outbound = lax.dynamic_index_in_dim(blocks, (tp_id + shift) % n_tp, 0, keepdims=False)
        summed = summed + lax.ppermute(
            outbound, "tp", [(t, (t + shift) % n_tp) for t in range(n_tp)]
        ).astype(jnp.float32)
    flat_stream = stream.reshape(rows_all, model_width)
    own_stream = lax.dynamic_slice_in_dim(flat_stream, tp_id * quarter, quarter, 0)
    post_rows = (own_stream.astype(jnp.float32) + summed).astype(jnp.bfloat16)
    post_float = post_rows.astype(jnp.float32)
    square = jnp.sum(post_float * post_float, axis=1)
    inverse = lax.rsqrt(square / model_width + EPS)
    normed = (post_float * inverse[:, None] * norm_gain[None, :]).astype(jnp.bfloat16)
    accept_own = lax.dynamic_slice_in_dim(
        lax.dynamic_index_in_dim(accept, own_slot, 0, keepdims=False), node_off, quarter, 1
    )
    picked_rows = jnp.dot(
        accept_own.astype(jnp.bfloat16), post_rows, preferred_element_type=jnp.float32
    ).astype(jnp.bfloat16)
    n_slots = dealing.shape[0]
    global_slot = req_id * slots + own_slot
    slot_ids = jnp.arange(n_slots, dtype=jnp.int32)
    owner = jnp.sum(jnp.where(slot_ids == global_slot, dealing, 0)) // slots
    dest_req = jnp.arange(n_req * n_tp, dtype=jnp.int32) // n_tp
    picked_parts = picked_rows.reshape(acc_rows, n_tp, dslice).transpose(1, 0, 2)
    picked_out = jnp.where(
        (dest_req == owner)[:, None, None],
        jnp.tile(picked_parts, (n_req, 1, 1)),
        jnp.zeros((), picked_parts.dtype),
    )
    picked_in = lax.all_to_all(
        picked_out, ("chip", "core", "tp"), split_axis=0, concat_axis=0, tiled=True
    )
    own_rows = lax.all_gather(normed, "chip", axis=0, tiled=True)
    partner_rows = lax.ppermute(
        own_rows, "core", [(c, (c + 1) % n_core) for c in range(n_core)]
    )
    vocab_loc = head_weight.shape[0]
    wanted = lax.dynamic_slice_in_dim(
        candidate.reshape(n_req, rows_all), tp_id * quarter, quarter, 1
    ).reshape(n_chip, n_core, quarter)
    vocab_ids = req_id * vocab_loc + jnp.arange(vocab_loc, dtype=jnp.int32)

    def block_stats(rows, core_of_rows):
        block_logits = lax.dot_general(
            rows, head_weight, (((1,), (1,)), ((), ())), preferred_element_type=jnp.float32
        )
        block_wanted = lax.dynamic_index_in_dim(wanted, core_of_rows, 1, keepdims=False)
        found = vocab_stats(block_logits, vocab_ids, block_wanted.reshape(-1), 1)
        return jnp.stack(found).reshape(3, n_chip, quarter)

    own_stats = block_stats(own_rows, core_id)
    partner_stats = block_stats(partner_rows, (core_id + n_core - 1) % n_core)
    serving_all = jnp.sum(
        jnp.where(dealing[None, :] == slot_ids[:, None], slot_ids[None, :], 0), axis=1
    )
    own_requests = req_id * slots + jnp.arange(slots, dtype=jnp.int32)
    own_serving = jnp.sum(
        jnp.where(dealing[None, :] == own_requests[:, None], slot_ids[None, :], 0), axis=1
    )
    source_slot = (
        jnp.arange(n_req * n_tp, dtype=jnp.int32) // n_tp * slots
        + jnp.arange(n_req * n_tp, dtype=jnp.int32) % n_tp // halves
    )
    source_request = jnp.sum(
        jnp.where(source_slot[:, None] == slot_ids[None, :], dealing[None, :], 0), axis=1
    )
    routed = source_request[None, :] == own_requests[:, None]
    accepted_state = jnp.einsum(
        "ks,sad->kad",
        routed.astype(jnp.bfloat16),
        picked_in,
        preferred_element_type=jnp.float32,
    ).astype(jnp.bfloat16)
    core_ids = jnp.arange(n_core, dtype=jnp.int32)
    local_stats = jnp.where(
        (core_ids == core_id)[None, :, None, None],
        own_stats.transpose(1, 0, 2)[:, None],
        partner_stats.transpose(1, 0, 2)[:, None],
    ).reshape(n_req, 3, quarter)
    dest_blocks = (serving_all // slots).reshape(n_req, 1, slots)
    dest_blocks = jnp.broadcast_to(dest_blocks, (n_req, n_tp, slots)).reshape(-1)
    block_ids = jnp.arange(n_req, dtype=jnp.int32)
    outgoing = jnp.sum(
        jnp.where(
            (dest_blocks[:, None] == block_ids[None, :])[:, :, None, None],
            local_stats[None],
            0.0,
        ),
        axis=1,
    ).reshape(n_req * n_tp, slots, 3, quarter)
    incoming = lax.all_to_all(
        outgoing, ("chip", "core", "tp"), split_axis=0, concat_axis=0, tiled=True
    ).reshape(n_req, n_tp, slots, 3, quarter)
    plane_of = (own_serving % slots)[:, None] * halves + jnp.arange(halves, dtype=jnp.int32)[None, :]
    plane_ids = jnp.arange(n_tp, dtype=jnp.int32)
    chosen = jnp.sum(
        jnp.where(
            (plane_of[:, :, None] == plane_ids[None, None, :])[None, :, :, :, None, None],
            incoming.transpose(0, 2, 1, 3, 4)[:, :, None],
            0.0,
        ),
        axis=3,
    )
    joint_max = jnp.max(chosen[:, :, :, 0], axis=0)
    joint_sum = jnp.sum(chosen[:, :, :, 1] * jnp.exp(chosen[:, :, :, 0] - joint_max[None]), axis=0)
    joint_pick = jnp.sum(chosen[:, :, :, 2], axis=0)
    target_logprob = (joint_pick - joint_max - jnp.log(joint_sum)).reshape(slots, tree_size)
    return (target_logprob, accepted_state)


def solution(mesh):
    n_req, n_tp = mesh.devices.shape
    fine = Mesh(mesh.devices.reshape(n_req // 2, 2, n_tp), ("chip", "core", "tp"))
    req = ("chip", "core")
    placed = (
        P(req, None, None),
        P(req, None, "tp"),
        P(req, None, "tp"),
        P(req, None, "tp"),
        P(req, None, "tp"),
        P(req, None, "tp"),
        P(req),
        P(req, None),
        P(req, None, None),
        P("tp", None),
        P(),
        P(req, None),
        P(),
        P(),
    )
    return jax.shard_map(
        local,
        mesh=fine,
        in_specs=placed,
        out_specs=(P(req, None), P(req, None, "tp")),
        check_vma=False,
    )
```

```python
import jax
import jax.numpy as jnp
from jax import lax
from jax.sharding import PartitionSpec as P

HD = 224
ACC = 8


EPS = 1e-05
HIGH = lax.Precision.HIGHEST
block_limit = 512


def combined_all(value, axis, join):
    pieces = jax.tree.map(lambda part: lax.all_gather(part, axis), value)
    head = jax.tree.map(lambda part: part[0], pieces)
    tail = jax.tree.map(lambda part: part[1:], pieces)
    subtotal, _ = lax.scan(lambda subtotal, share: (join(subtotal, share), None), head, tail)
    return subtotal


def ancestry(parents):
    node_count = parents.shape[-1]
    node_ids = jnp.arange(node_count, dtype=jnp.int32)
    stride_map = (parents[..., :, None] == node_ids).astype(jnp.float32)
    reached = jnp.broadcast_to(jnp.eye(node_count, dtype=jnp.float32), stride_map.shape) > 0.5
    for doubling in range((ACC - 1).bit_length()):
        further = lax.optimization_barrier(
            jnp.einsum("rtk,rku->rtu", reached.astype(jnp.float32), stride_map, precision=HIGH)
        )
        reached = jnp.logical_or(reached, further > 0.5)
        stride_map = jnp.einsum("rtk,rku->rtu", stride_map, stride_map, precision=HIGH)
    return reached


def combine_stats(earlier, later):
    joint_max = jnp.maximum(earlier[0], later[0])
    joint_sum = earlier[1] * jnp.exp(earlier[0] - joint_max) + later[1] * jnp.exp(
        later[0] - joint_max
    )
    return (joint_max, joint_sum, earlier[2] + later[2])


def vocab_stats(logits, vocab_ids, wanted, along):
    row_max = jnp.max(logits, axis=along)
    row_sum = jnp.sum(jnp.exp(logits - jnp.expand_dims(row_max, along)), axis=along)
    matches = jnp.expand_dims(vocab_ids, 1 - along) == jnp.expand_dims(wanted, along)
    picked = jnp.sum(jnp.where(matches, logits, 0.0), axis=along)
    return (row_max, row_sum, picked)


def local(
    stream,
    queries,
    key_new,
    value_new,
    cache_key,
    cache_value,
    cache_length,
    parents,
    accept,
    out_weight,
    norm_gain,
    head_weight,
    candidate,
    dealing,
):
    slots, tree_size, qwidth = queries.shape
    model_width = stream.shape[2]
    heads_loc = qwidth // HD
    n_tp = lax.axis_size("tp")
    n_req = lax.axis_size("req")
    tp_id = lax.axis_index("tp")
    req_id = lax.axis_index("req")
    score_scale = HD ** (-0.5)
    cache_cap = cache_key.shape[1]
    column_head = jnp.arange(qwidth, dtype=jnp.int32) // HD
    head_mask = column_head[None, :] == jnp.arange(heads_loc, dtype=jnp.int32)[:, None]
    spread_q = jnp.where(
        head_mask[None, :, None, :], queries[:, None, :, :], jnp.zeros((), queries.dtype)
    ).reshape(slots, heads_loc * tree_size, qwidth)
    past_scores = (
        jnp.einsum("rnd,rkd->rnk", spread_q, cache_key, preferred_element_type=jnp.float32)
        * score_scale
    )
    live = jnp.arange(cache_cap, dtype=jnp.int32)[None, :] < cache_length[:, None]
    past_scores = jnp.where(live[:, None, :], past_scores, -jnp.inf)
    visible = ancestry(parents)
    seen = jnp.broadcast_to(
        visible[:, None], (slots, heads_loc, tree_size, tree_size)
    ).reshape(slots, heads_loc * tree_size, tree_size)
    tree_scores = (
        jnp.einsum("rnd,rkd->rnk", spread_q, key_new, preferred_element_type=jnp.float32)
        * score_scale
    )
    tree_scores = jnp.where(seen, tree_scores, -jnp.inf)
    highest = jnp.maximum(jnp.max(past_scores, axis=2), jnp.max(tree_scores, axis=2))
    past_weights = jnp.exp(past_scores - highest[..., None])
    tree_weights = jnp.exp(tree_scores - highest[..., None])
    denominator = jnp.sum(past_weights, axis=2) + jnp.sum(tree_weights, axis=2)
    mixed = jnp.einsum(
        "rnk,rkd->rnd",
        past_weights.astype(jnp.bfloat16),
        cache_value,
        preferred_element_type=jnp.float32,
    ) + jnp.einsum(
        "rnk,rkd->rnd",
        tree_weights.astype(jnp.bfloat16),
        value_new,
        preferred_element_type=jnp.float32,
    )
    mixed = (mixed / denominator[..., None]).reshape(slots, heads_loc, tree_size, qwidth)
    attention = jnp.sum(
        jnp.where(head_mask[None, :, None, :], mixed, 0.0), axis=1
    ).astype(jnp.bfloat16)
    attention_rows = attention.reshape(slots * tree_size, qwidth)
    rows_all = slots * tree_size
    quarter = rows_all // n_tp
    dslice = model_width // n_tp
    halves = tree_size // quarter
    acc_rows = accept.shape[1]
    own_slot = tp_id // halves
    node_off = (tp_id % halves) * quarter
    partial_out = jnp.dot(
        attention_rows, out_weight, preferred_element_type=jnp.float32
    ).astype(jnp.bfloat16)
    blocks = partial_out.reshape(n_tp, quarter, model_width)
    summed = lax.dynamic_index_in_dim(blocks, tp_id, 0, keepdims=False).astype(jnp.float32)
    for shift in range(1, n_tp):
        outbound = lax.dynamic_index_in_dim(blocks, (tp_id + shift) % n_tp, 0, keepdims=False)
        summed = summed + lax.ppermute(
            outbound, "tp", [(t, (t + shift) % n_tp) for t in range(n_tp)]
        ).astype(jnp.float32)
    flat_stream = stream.reshape(rows_all, model_width)
    own_stream = lax.dynamic_slice_in_dim(flat_stream, tp_id * quarter, quarter, 0)
    post_rows = (own_stream.astype(jnp.float32) + summed).astype(jnp.bfloat16)
    post_float = post_rows.astype(jnp.float32)
    square = jnp.sum(post_float * post_float, axis=1)
    inverse = lax.rsqrt(square / model_width + EPS)
    normed = (post_float * inverse[:, None] * norm_gain[None, :]).astype(jnp.bfloat16)
    accept_own = lax.dynamic_slice_in_dim(
        lax.dynamic_index_in_dim(accept, own_slot, 0, keepdims=False), node_off, quarter, 1
    )
    picked_rows = jnp.dot(
        accept_own.astype(jnp.bfloat16), post_rows, preferred_element_type=jnp.float32
    ).astype(jnp.bfloat16)
    n_slots = dealing.shape[0]
    slot_ids = jnp.arange(n_slots, dtype=jnp.int32)
    picked_parts = picked_rows.reshape(acc_rows, n_tp, dslice).transpose(1, 0, 2)
    parts_in = lax.all_to_all(picked_parts, "tp", split_axis=0, concat_axis=0, tiled=True)
    plane_slot = jnp.arange(n_tp, dtype=jnp.int32) // halves
    local_slots = jnp.arange(slots, dtype=jnp.int32)
    compact = jnp.einsum(
        "lt,tad->lad",
        (plane_slot[None, :] == local_slots[:, None]).astype(jnp.bfloat16),
        parts_in,
        preferred_element_type=jnp.float32,
    ).astype(jnp.bfloat16)
    my_slots = req_id * slots + local_slots
    my_requests = jnp.sum(
        jnp.where(slot_ids[None, :] == my_slots[:, None], dealing[None, :], 0), axis=1
    )
    dest_ids = jnp.arange(n_req, dtype=jnp.int32)
    compact_out = jnp.where(
        ((my_requests // slots)[None, :] == dest_ids[:, None])[:, :, None, None],
        compact[None],
        jnp.zeros((), compact.dtype),
    )
    compact_in = lax.all_to_all(compact_out, "req", split_axis=0, concat_axis=0, tiled=True)
    all_rows = lax.all_gather(normed, "req", axis=0, tiled=True)
    vocab_loc = head_weight.shape[0]
    wanted_rows = lax.dynamic_slice_in_dim(
        candidate.reshape(n_req, rows_all), tp_id * quarter, quarter, 1
    ).reshape(-1)
    vocab_ids = req_id * vocab_loc + jnp.arange(vocab_loc, dtype=jnp.int32)
    logits = lax.dot_general(
        all_rows, head_weight, (((1,), (1,)), ((), ())), preferred_element_type=jnp.float32
    )
    serving_all = jnp.sum(
        jnp.where(dealing[None, :] == slot_ids[:, None], slot_ids[None, :], 0), axis=1
    )
    own_requests = req_id * slots + jnp.arange(slots, dtype=jnp.int32)
    own_serving = jnp.sum(
        jnp.where(dealing[None, :] == own_requests[:, None], slot_ids[None, :], 0), axis=1
    )
    routed = dealing[None, :] == own_requests[:, None]
    accepted_state = jnp.einsum(
        "ks,sad->kad",
        routed.astype(jnp.bfloat16),
        compact_in.reshape(n_slots, acc_rows, dslice),
        preferred_element_type=jnp.float32,
    ).astype(jnp.bfloat16)
    row_max, row_sum, picked = vocab_stats(logits, vocab_ids, wanted_rows, 1)
    local_stats = jnp.stack([row_max, row_sum, picked]).reshape(3, n_req, quarter)
    local_stats = local_stats.transpose(1, 0, 2)
    dest_blocks = (serving_all // slots).reshape(n_req, 1, slots)
    dest_blocks = jnp.broadcast_to(dest_blocks, (n_req, n_tp, slots)).reshape(-1)
    block_ids = jnp.arange(n_req, dtype=jnp.int32)
    outgoing = jnp.sum(
        jnp.where(
            (dest_blocks[:, None] == block_ids[None, :])[:, :, None, None],
            local_stats[None],
            0.0,
        ),
        axis=1,
    ).reshape(n_req * n_tp, slots, 3, quarter)
    incoming = lax.all_to_all(
        outgoing, ("req", "tp"), split_axis=0, concat_axis=0, tiled=True
    ).reshape(n_req, n_tp, slots, 3, quarter)
    plane_of = (own_serving % slots)[:, None] * halves + jnp.arange(halves, dtype=jnp.int32)[None, :]
    plane_ids = jnp.arange(n_tp, dtype=jnp.int32)
    chosen = jnp.sum(
        jnp.where(
            (plane_of[:, :, None] == plane_ids[None, None, :])[None, :, :, :, None, None],
            incoming.transpose(0, 2, 1, 3, 4)[:, :, None],
            0.0,
        ),
        axis=3,
    )
    joint_max = jnp.max(chosen[:, :, :, 0], axis=0)
    joint_sum = jnp.sum(chosen[:, :, :, 1] * jnp.exp(chosen[:, :, :, 0] - joint_max[None]), axis=0)
    joint_pick = jnp.sum(chosen[:, :, :, 2], axis=0)
    target_logprob = (joint_pick - joint_max - jnp.log(joint_sum)).reshape(slots, tree_size)
    return (target_logprob, accepted_state)


def solution(mesh):
    placed = (
        P("req", None, None),
        P("req", None, "tp"),
        P("req", None, "tp"),
        P("req", None, "tp"),
        P("req", None, "tp"),
        P("req", None, "tp"),
        P("req"),
        P("req", None),
        P("req", None, None),
        P("tp", None),
        P(),
        P("req", None),
        P(),
        P(),
    )
    return jax.shard_map(
        local,
        mesh=mesh,
        in_specs=placed,
        out_specs=(P("req", None), P("req", None, "tp")),
        check_vma=False,
    )
```

```python
import jax
import jax.numpy as jnp
from jax import lax
from jax.sharding import PartitionSpec as P

HD = 224
ACC = 8


EPS = 1e-05
HIGH = lax.Precision.HIGHEST
block_limit = 512


def combined_all(value, axis, join):
    pieces = jax.tree.map(lambda part: lax.all_gather(part, axis), value)
    head = jax.tree.map(lambda part: part[0], pieces)
    tail = jax.tree.map(lambda part: part[1:], pieces)
    subtotal, _ = lax.scan(lambda subtotal, share: (join(subtotal, share), None), head, tail)
    return subtotal


def ancestry(parents):
    node_count = parents.shape[-1]
    node_ids = jnp.arange(node_count, dtype=jnp.int32)
    stride_map = (parents[..., :, None] == node_ids).astype(jnp.bfloat16)
    reached = jnp.broadcast_to(jnp.eye(node_count, dtype=jnp.bool_), stride_map.shape)
    for doubling in range((ACC - 1).bit_length()):
        further = jnp.einsum(
            "rtk,rku->rtu",
            reached.astype(jnp.bfloat16),
            stride_map,
            preferred_element_type=jnp.float32,
        )
        reached = jnp.logical_or(reached, further > 0.5)
        stride_map = (
            jnp.einsum("rtk,rku->rtu", stride_map, stride_map, preferred_element_type=jnp.float32)
            > 0.5
        ).astype(jnp.bfloat16)
    return reached


def combine_stats(earlier, later):
    joint_max = jnp.maximum(earlier[0], later[0])
    joint_sum = earlier[1] * jnp.exp(earlier[0] - joint_max) + later[1] * jnp.exp(
        later[0] - joint_max
    )
    return (joint_max, joint_sum, earlier[2] + later[2])


def vocab_stats(logits, vocab_ids, wanted, along):
    row_max = jnp.max(logits, axis=along)
    row_sum = jnp.sum(jnp.exp(logits - jnp.expand_dims(row_max, along)), axis=along)
    matches = jnp.expand_dims(vocab_ids, 1 - along) == jnp.expand_dims(wanted, along)
    picked = jnp.sum(jnp.where(matches, logits, 0.0), axis=along)
    return (row_max, row_sum, picked)


def local(
    stream,
    queries,
    key_new,
    value_new,
    cache_key,
    cache_value,
    cache_length,
    parents,
    accept,
    out_weight,
    norm_gain,
    head_weight,
    candidate,
    dealing,
):
    slots, tree_size, qwidth = queries.shape
    model_width = stream.shape[2]
    heads_loc = qwidth // HD
    n_tp = lax.axis_size("tp")
    n_req = lax.axis_size("req")
    tp_id = lax.axis_index("tp")
    req_id = lax.axis_index("req")
    score_scale = HD ** (-0.5)
    cache_cap = cache_key.shape[1]
    column_head = jnp.arange(qwidth, dtype=jnp.int32) // HD
    head_mask = column_head[None, :] == jnp.arange(heads_loc, dtype=jnp.int32)[:, None]
    spread_q = jnp.where(
        head_mask[None, :, None, :], queries[:, None, :, :], jnp.zeros((), queries.dtype)
    ).reshape(slots, heads_loc * tree_size, qwidth)
    past_scores = (
        jnp.einsum("rnd,rkd->rnk", spread_q, cache_key, preferred_element_type=jnp.float32)
        * score_scale
    )
    live = jnp.arange(cache_cap, dtype=jnp.int32)[None, :] < cache_length[:, None]
    past_scores = jnp.where(live[:, None, :], past_scores, -jnp.inf)
    visible = ancestry(parents)
    seen = jnp.broadcast_to(
        visible[:, None], (slots, heads_loc, tree_size, tree_size)
    ).reshape(slots, heads_loc * tree_size, tree_size)
    tree_scores = (
        jnp.einsum("rnd,rkd->rnk", spread_q, key_new, preferred_element_type=jnp.float32)
        * score_scale
    )
    tree_scores = jnp.where(seen, tree_scores, -jnp.inf)
    highest = jnp.maximum(jnp.max(past_scores, axis=2), jnp.max(tree_scores, axis=2))
    past_weights = jnp.exp(past_scores - highest[..., None])
    tree_weights = jnp.exp(tree_scores - highest[..., None])
    denominator = jnp.sum(past_weights, axis=2) + jnp.sum(tree_weights, axis=2)
    mixed = jnp.einsum(
        "rnk,rkd->rnd",
        past_weights.astype(jnp.bfloat16),
        cache_value,
        preferred_element_type=jnp.float32,
    ) + jnp.einsum(
        "rnk,rkd->rnd",
        tree_weights.astype(jnp.bfloat16),
        value_new,
        preferred_element_type=jnp.float32,
    )
    mixed = (mixed / denominator[..., None]).reshape(slots, heads_loc, tree_size, qwidth)
    attention = jnp.sum(
        jnp.where(head_mask[None, :, None, :], mixed, 0.0), axis=1
    ).astype(jnp.bfloat16)
    attention_rows = attention.reshape(slots * tree_size, qwidth)
    rows_all = slots * tree_size
    quarter = rows_all // n_tp
    dslice = model_width // n_tp
    halves = tree_size // quarter
    acc_rows = accept.shape[1]
    own_slot = tp_id // halves
    node_off = (tp_id % halves) * quarter
    def partial_block(owner_tp):
        block_rows = lax.dynamic_slice_in_dim(attention_rows, owner_tp * quarter, quarter, 0)
        return jnp.dot(
            block_rows, out_weight, preferred_element_type=jnp.float32
        ).astype(jnp.bfloat16)

    arrived = []
    for shift in range(1, n_tp):
        outbound = partial_block((tp_id + shift) % n_tp)
        arrived.append(
            lax.ppermute(outbound, "tp", [(t, (t + shift) % n_tp) for t in range(n_tp)])
        )
    summed = partial_block(tp_id).astype(jnp.float32)
    for block in arrived:
        summed = summed + block.astype(jnp.float32)
    flat_stream = stream.reshape(rows_all, model_width)
    own_stream = lax.dynamic_slice_in_dim(flat_stream, tp_id * quarter, quarter, 0)
    post_rows = (own_stream.astype(jnp.float32) + summed).astype(jnp.bfloat16)
    post_float = post_rows.astype(jnp.float32)
    square = jnp.sum(post_float * post_float, axis=1)
    inverse = lax.rsqrt(square / model_width + EPS)
    normed = (post_float * inverse[:, None] * norm_gain[None, :]).astype(jnp.bfloat16)
    accept_own = lax.dynamic_slice_in_dim(
        lax.dynamic_index_in_dim(accept, own_slot, 0, keepdims=False), node_off, quarter, 1
    )
    picked_rows = jnp.dot(
        accept_own.astype(jnp.bfloat16), post_rows, preferred_element_type=jnp.float32
    ).astype(jnp.bfloat16)
    n_slots = dealing.shape[0]
    slot_ids = jnp.arange(n_slots, dtype=jnp.int32)
    picked_parts = picked_rows.reshape(acc_rows, n_tp, dslice).transpose(1, 0, 2)
    parts_in = lax.all_to_all(picked_parts, "tp", split_axis=0, concat_axis=0, tiled=True)
    plane_slot = jnp.arange(n_tp, dtype=jnp.int32) // halves
    local_slots = jnp.arange(slots, dtype=jnp.int32)
    compact = jnp.einsum(
        "lt,tad->lad",
        (plane_slot[None, :] == local_slots[:, None]).astype(jnp.bfloat16),
        parts_in,
        preferred_element_type=jnp.float32,
    ).astype(jnp.bfloat16)
    my_slots = req_id * slots + local_slots
    my_requests = jnp.sum(
        jnp.where(slot_ids[None, :] == my_slots[:, None], dealing[None, :], 0), axis=1
    )
    dest_ids = jnp.arange(n_req, dtype=jnp.int32)
    compact_out = jnp.where(
        ((my_requests // slots)[None, :] == dest_ids[:, None])[:, :, None, None],
        compact[None],
        jnp.zeros((), compact.dtype),
    )
    compact_in = lax.all_to_all(compact_out, "req", split_axis=0, concat_axis=0, tiled=True)
    all_rows = lax.all_gather(normed, "req", axis=0, tiled=True)
    vocab_loc = head_weight.shape[0]
    wanted_rows = lax.dynamic_slice_in_dim(
        candidate.reshape(n_req, rows_all), tp_id * quarter, quarter, 1
    ).reshape(-1)
    vocab_ids = req_id * vocab_loc + jnp.arange(vocab_loc, dtype=jnp.int32)
    logits = lax.dot_general(
        all_rows, head_weight, (((1,), (1,)), ((), ())), preferred_element_type=jnp.float32
    )
    serving_all = jnp.sum(
        jnp.where(dealing[None, :] == slot_ids[:, None], slot_ids[None, :], 0), axis=1
    )
    own_requests = req_id * slots + jnp.arange(slots, dtype=jnp.int32)
    own_serving = jnp.sum(
        jnp.where(dealing[None, :] == own_requests[:, None], slot_ids[None, :], 0), axis=1
    )
    routed = dealing[None, :] == own_requests[:, None]
    accepted_state = jnp.einsum(
        "ks,sad->kad",
        routed.astype(jnp.bfloat16),
        compact_in.reshape(n_slots, acc_rows, dslice),
        preferred_element_type=jnp.float32,
    ).astype(jnp.bfloat16)
    row_max, row_sum, picked = vocab_stats(logits, vocab_ids, wanted_rows, 1)
    local_stats = jnp.stack([row_max, row_sum, picked]).reshape(3, n_req, quarter)
    local_stats = local_stats.transpose(1, 0, 2)
    dest_blocks = (serving_all // slots).reshape(n_req, 1, slots)
    dest_blocks = jnp.broadcast_to(dest_blocks, (n_req, n_tp, slots)).reshape(-1)
    block_ids = jnp.arange(n_req, dtype=jnp.int32)
    outgoing = jnp.sum(
        jnp.where(
            (dest_blocks[:, None] == block_ids[None, :])[:, :, None, None],
            local_stats[None],
            0.0,
        ),
        axis=1,
    ).reshape(n_req * n_tp, slots, 3, quarter)
    incoming = lax.all_to_all(
        outgoing, ("req", "tp"), split_axis=0, concat_axis=0, tiled=True
    ).reshape(n_req, n_tp, slots, 3, quarter)
    plane_of = (own_serving % slots)[:, None] * halves + jnp.arange(halves, dtype=jnp.int32)[None, :]
    plane_ids = jnp.arange(n_tp, dtype=jnp.int32)
    chosen = jnp.sum(
        jnp.where(
            (plane_of[:, :, None] == plane_ids[None, None, :])[None, :, :, :, None, None],
            incoming.transpose(0, 2, 1, 3, 4)[:, :, None],
            0.0,
        ),
        axis=3,
    )
    joint_max = jnp.max(chosen[:, :, :, 0], axis=0)
    joint_sum = jnp.sum(chosen[:, :, :, 1] * jnp.exp(chosen[:, :, :, 0] - joint_max[None]), axis=0)
    joint_pick = jnp.sum(chosen[:, :, :, 2], axis=0)
    target_logprob = (joint_pick - joint_max - jnp.log(joint_sum)).reshape(slots, tree_size)
    return (target_logprob, accepted_state)


def solution(mesh):
    placed = (
        P("req", None, None),
        P("req", None, "tp"),
        P("req", None, "tp"),
        P("req", None, "tp"),
        P("req", None, "tp"),
        P("req", None, "tp"),
        P("req"),
        P("req", None),
        P("req", None, None),
        P("tp", None),
        P(),
        P("req", None),
        P(),
        P(),
    )
    return jax.shard_map(
        local,
        mesh=mesh,
        in_specs=placed,
        out_specs=(P("req", None), P("req", None, "tp")),
        check_vma=False,
    )
```

```python
import jax
import jax.numpy as jnp
from jax import lax
from jax.sharding import PartitionSpec as P

HD = 224
ACC = 8


EPS = 1e-05
HIGH = lax.Precision.HIGHEST
block_limit = 512


def combined_all(value, axis, join):
    pieces = jax.tree.map(lambda part: lax.all_gather(part, axis), value)
    head = jax.tree.map(lambda part: part[0], pieces)
    tail = jax.tree.map(lambda part: part[1:], pieces)
    subtotal, _ = lax.scan(lambda subtotal, share: (join(subtotal, share), None), head, tail)
    return subtotal


def ancestry(parents):
    node_count = parents.shape[-1]
    node_ids = jnp.arange(node_count, dtype=jnp.int32)
    stride_map = (parents[..., :, None] == node_ids).astype(jnp.float32)
    reached = jnp.broadcast_to(jnp.eye(node_count, dtype=jnp.float32), stride_map.shape) > 0.5
    for doubling in range((ACC - 1).bit_length()):
        further = lax.optimization_barrier(
            jnp.einsum("rtk,rku->rtu", reached.astype(jnp.float32), stride_map, precision=HIGH)
        )
        reached = jnp.logical_or(reached, further > 0.5)
        stride_map = jnp.einsum("rtk,rku->rtu", stride_map, stride_map, precision=HIGH)
    return reached


def combine_stats(earlier, later):
    joint_max = jnp.maximum(earlier[0], later[0])
    joint_sum = earlier[1] * jnp.exp(earlier[0] - joint_max) + later[1] * jnp.exp(
        later[0] - joint_max
    )
    return (joint_max, joint_sum, earlier[2] + later[2])


def vocab_stats(logits, vocab_ids, wanted, along):
    row_max = jnp.max(logits, axis=along)
    row_sum = jnp.sum(jnp.exp(logits - jnp.expand_dims(row_max, along)), axis=along)
    matches = jnp.expand_dims(vocab_ids, 1 - along) == jnp.expand_dims(wanted, along)
    picked = jnp.sum(jnp.where(matches, logits, 0.0), axis=along)
    return (row_max, row_sum, picked)


def local(
    stream,
    queries,
    key_new,
    value_new,
    cache_key,
    cache_value,
    cache_length,
    parents,
    accept,
    out_weight,
    norm_gain,
    head_weight,
    candidate,
    dealing,
):
    slots, tree_size, qwidth = queries.shape
    model_width = stream.shape[2]
    heads_loc = qwidth // HD
    n_tp = lax.axis_size("tp")
    n_req = lax.axis_size("req")
    tp_id = lax.axis_index("tp")
    req_id = lax.axis_index("req")
    score_scale = HD ** (-0.5)
    cache_cap = cache_key.shape[1]
    column_head = jnp.arange(qwidth, dtype=jnp.int32) // HD
    head_mask = column_head[None, :] == jnp.arange(heads_loc, dtype=jnp.int32)[:, None]
    spread_q = jnp.where(
        head_mask[None, :, None, :], queries[:, None, :, :], jnp.zeros((), queries.dtype)
    ).reshape(slots, heads_loc * tree_size, qwidth)
    past_scores = (
        jnp.einsum("rnd,rkd->rnk", spread_q, cache_key, preferred_element_type=jnp.float32)
        * score_scale
    )
    live = jnp.arange(cache_cap, dtype=jnp.int32)[None, :] < cache_length[:, None]
    past_scores = jnp.where(live[:, None, :], past_scores, -jnp.inf)
    visible = ancestry(parents)
    seen = jnp.broadcast_to(
        visible[:, None], (slots, heads_loc, tree_size, tree_size)
    ).reshape(slots, heads_loc * tree_size, tree_size)
    tree_scores = (
        jnp.einsum("rnd,rkd->rnk", spread_q, key_new, preferred_element_type=jnp.float32)
        * score_scale
    )
    tree_scores = jnp.where(seen, tree_scores, -jnp.inf)
    highest = jnp.maximum(jnp.max(past_scores, axis=2), jnp.max(tree_scores, axis=2))
    past_weights = jnp.exp(past_scores - highest[..., None])
    tree_weights = jnp.exp(tree_scores - highest[..., None])
    denominator = jnp.sum(past_weights, axis=2) + jnp.sum(tree_weights, axis=2)
    mixed = jnp.einsum(
        "rnk,rkd->rnd",
        past_weights.astype(jnp.bfloat16),
        cache_value,
        preferred_element_type=jnp.float32,
    ) + jnp.einsum(
        "rnk,rkd->rnd",
        tree_weights.astype(jnp.bfloat16),
        value_new,
        preferred_element_type=jnp.float32,
    )
    mixed = (mixed / denominator[..., None]).reshape(slots, heads_loc, tree_size, qwidth)
    attention = jnp.sum(
        jnp.where(head_mask[None, :, None, :], mixed, 0.0), axis=1
    ).astype(jnp.bfloat16)
    attention_rows = attention.reshape(slots * tree_size, qwidth)
    rows_all = slots * tree_size
    quarter = rows_all // n_tp
    dslice = model_width // n_tp
    halves = tree_size // quarter
    acc_rows = accept.shape[1]
    own_slot = tp_id // halves
    node_off = (tp_id % halves) * quarter
    partial_out = jnp.dot(
        attention_rows, out_weight, preferred_element_type=jnp.float32
    ).astype(jnp.bfloat16)
    blocks = partial_out.reshape(n_tp, quarter, model_width)
    summed = lax.dynamic_index_in_dim(blocks, tp_id, 0, keepdims=False).astype(jnp.float32)
    for shift in range(1, n_tp):
        outbound = lax.dynamic_index_in_dim(blocks, (tp_id + shift) % n_tp, 0, keepdims=False)
        summed = summed + lax.ppermute(
            outbound, "tp", [(t, (t + shift) % n_tp) for t in range(n_tp)]
        ).astype(jnp.float32)
    flat_stream = stream.reshape(rows_all, model_width)
    own_stream = lax.dynamic_slice_in_dim(flat_stream, tp_id * quarter, quarter, 0)
    post_rows = (own_stream.astype(jnp.float32) + summed).astype(jnp.bfloat16)
    post_float = post_rows.astype(jnp.float32)
    square = jnp.sum(post_float * post_float, axis=1)
    inverse = lax.rsqrt(square / model_width + EPS)
    normed = (post_float * inverse[:, None] * norm_gain[None, :]).astype(jnp.bfloat16)
    accept_own = lax.dynamic_slice_in_dim(
        lax.dynamic_index_in_dim(accept, own_slot, 0, keepdims=False), node_off, quarter, 1
    )
    picked_rows = jnp.dot(
        accept_own.astype(jnp.bfloat16), post_rows, preferred_element_type=jnp.float32
    ).astype(jnp.bfloat16)
    n_slots = dealing.shape[0]
    slot_ids = jnp.arange(n_slots, dtype=jnp.int32)
    picked_parts = picked_rows.reshape(acc_rows, n_tp, dslice).transpose(1, 0, 2)
    parts_in = lax.all_to_all(picked_parts, "tp", split_axis=0, concat_axis=0, tiled=True)
    plane_slot = jnp.arange(n_tp, dtype=jnp.int32) // halves
    local_slots = jnp.arange(slots, dtype=jnp.int32)
    compact = jnp.einsum(
        "lt,tad->lad",
        (plane_slot[None, :] == local_slots[:, None]).astype(jnp.bfloat16),
        parts_in,
        preferred_element_type=jnp.float32,
    ).astype(jnp.bfloat16)
    my_slots = req_id * slots + local_slots
    my_requests = jnp.sum(
        jnp.where(slot_ids[None, :] == my_slots[:, None], dealing[None, :], 0), axis=1
    )
    dest_ids = jnp.arange(n_req, dtype=jnp.int32)
    compact_out = jnp.where(
        ((my_requests // slots)[None, :] == dest_ids[:, None])[:, :, None, None],
        compact[None],
        jnp.zeros((), compact.dtype),
    )
    compact_in = lax.all_to_all(
        compact_out.reshape(n_req, slots * acc_rows, dslice),
        "req",
        split_axis=0,
        concat_axis=0,
        tiled=True,
    )
    all_rows = lax.all_gather(normed, "req", axis=0, tiled=True)
    vocab_loc = head_weight.shape[0]
    wanted_rows = lax.dynamic_slice_in_dim(
        candidate.reshape(n_req, rows_all), tp_id * quarter, quarter, 1
    ).reshape(-1)
    vocab_ids = req_id * vocab_loc + jnp.arange(vocab_loc, dtype=jnp.int32)
    logits = lax.dot_general(
        all_rows, head_weight, (((1,), (1,)), ((), ())), preferred_element_type=jnp.float32
    )
    serving_all = jnp.sum(
        jnp.where(dealing[None, :] == slot_ids[:, None], slot_ids[None, :], 0), axis=1
    )
    own_requests = req_id * slots + jnp.arange(slots, dtype=jnp.int32)
    own_serving = jnp.sum(
        jnp.where(dealing[None, :] == own_requests[:, None], slot_ids[None, :], 0), axis=1
    )
    routed = dealing[None, :] == own_requests[:, None]
    accepted_state = jnp.einsum(
        "ks,sad->kad",
        routed.astype(jnp.bfloat16),
        compact_in.reshape(n_slots, acc_rows, dslice),
        preferred_element_type=jnp.float32,
    ).astype(jnp.bfloat16)
    row_max, row_sum, picked = vocab_stats(logits, vocab_ids, wanted_rows, 1)
    local_stats = jnp.stack([row_max, row_sum, picked]).reshape(3, n_req, quarter)
    local_stats = local_stats.transpose(1, 0, 2)
    dest_blocks = (serving_all // slots).reshape(n_req, 1, slots)
    dest_blocks = jnp.broadcast_to(dest_blocks, (n_req, n_tp, slots)).reshape(-1)
    block_ids = jnp.arange(n_req, dtype=jnp.int32)
    outgoing = jnp.sum(
        jnp.where(
            (dest_blocks[:, None] == block_ids[None, :])[:, :, None, None],
            local_stats[None],
            0.0,
        ),
        axis=1,
    ).reshape(n_req * n_tp, slots, 3, quarter)
    incoming = lax.all_to_all(
        outgoing.reshape(n_req * n_tp, slots * 3 * quarter),
        ("req", "tp"),
        split_axis=0,
        concat_axis=0,
        tiled=True,
    ).reshape(n_req, n_tp, slots, 3, quarter)
    plane_of = (own_serving % slots)[:, None] * halves + jnp.arange(halves, dtype=jnp.int32)[None, :]
    plane_ids = jnp.arange(n_tp, dtype=jnp.int32)
    chosen = jnp.sum(
        jnp.where(
            (plane_of[:, :, None] == plane_ids[None, None, :])[None, :, :, :, None, None],
            incoming.transpose(0, 2, 1, 3, 4)[:, :, None],
            0.0,
        ),
        axis=3,
    )
    joint_max = jnp.max(chosen[:, :, :, 0], axis=0)
    joint_sum = jnp.sum(chosen[:, :, :, 1] * jnp.exp(chosen[:, :, :, 0] - joint_max[None]), axis=0)
    joint_pick = jnp.sum(chosen[:, :, :, 2], axis=0)
    target_logprob = (joint_pick - joint_max - jnp.log(joint_sum)).reshape(slots, tree_size)
    return (target_logprob, accepted_state)


def solution(mesh):
    placed = (
        P("req", None, None),
        P("req", None, "tp"),
        P("req", None, "tp"),
        P("req", None, "tp"),
        P("req", None, "tp"),
        P("req", None, "tp"),
        P("req"),
        P("req", None),
        P("req", None, None),
        P("tp", None),
        P(),
        P("req", None),
        P(),
        P(),
    )
    return jax.shard_map(
        local,
        mesh=mesh,
        in_specs=placed,
        out_specs=(P("req", None), P("req", None, "tp")),
        check_vma=False,
    )
```

```python
import jax
import jax.numpy as jnp
from jax import lax
from jax.sharding import PartitionSpec as P

HD = 224
ACC = 8


EPS = 1e-05
HIGH = lax.Precision.HIGHEST
block_limit = 512


def combined_all(value, axis, join):
    pieces = jax.tree.map(lambda part: lax.all_gather(part, axis), value)
    head = jax.tree.map(lambda part: part[0], pieces)
    tail = jax.tree.map(lambda part: part[1:], pieces)
    subtotal, _ = lax.scan(lambda subtotal, share: (join(subtotal, share), None), head, tail)
    return subtotal


def ancestry(parents):
    node_count = parents.shape[-1]
    node_ids = jnp.arange(node_count, dtype=jnp.int32)
    stride_map = (parents[..., :, None] == node_ids).astype(jnp.float32)
    reached = jnp.broadcast_to(jnp.eye(node_count, dtype=jnp.float32), stride_map.shape) > 0.5
    for doubling in range((ACC - 1).bit_length()):
        further = lax.optimization_barrier(
            jnp.einsum("rtk,rku->rtu", reached.astype(jnp.float32), stride_map, precision=HIGH)
        )
        reached = jnp.logical_or(reached, further > 0.5)
        stride_map = jnp.einsum("rtk,rku->rtu", stride_map, stride_map, precision=HIGH)
    return reached


def combine_stats(earlier, later):
    joint_max = jnp.maximum(earlier[0], later[0])
    joint_sum = earlier[1] * jnp.exp(earlier[0] - joint_max) + later[1] * jnp.exp(
        later[0] - joint_max
    )
    return (joint_max, joint_sum, earlier[2] + later[2])


def vocab_stats(logits, vocab_ids, wanted, along):
    row_max = jnp.max(logits, axis=along)
    row_sum = jnp.sum(jnp.exp(logits - jnp.expand_dims(row_max, along)), axis=along)
    matches = jnp.expand_dims(vocab_ids, 1 - along) == jnp.expand_dims(wanted, along)
    picked = jnp.sum(jnp.where(matches, logits, 0.0), axis=along)
    return (row_max, row_sum, picked)


def local(
    stream,
    queries,
    key_new,
    value_new,
    cache_key,
    cache_value,
    cache_length,
    parents,
    accept,
    out_weight,
    norm_gain,
    head_weight,
    candidate,
    dealing,
):
    slots, tree_size, qwidth = queries.shape
    model_width = stream.shape[2]
    heads_loc = qwidth // HD
    n_tp = lax.axis_size("tp")
    n_req = lax.axis_size("req")
    tp_id = lax.axis_index("tp")
    req_id = lax.axis_index("req")
    score_scale = HD ** (-0.5)
    cache_cap = cache_key.shape[1]
    column_head = jnp.arange(qwidth, dtype=jnp.int32) // HD
    head_mask = column_head[None, :] == jnp.arange(heads_loc, dtype=jnp.int32)[:, None]
    spread_q = jnp.where(
        head_mask[None, :, None, :], queries[:, None, :, :], jnp.zeros((), queries.dtype)
    ).reshape(slots, heads_loc * tree_size, qwidth)
    past_scores = (
        jnp.einsum("rnd,rkd->rnk", spread_q, cache_key, preferred_element_type=jnp.float32)
        * score_scale
    )
    live = jnp.arange(cache_cap, dtype=jnp.int32)[None, :] < cache_length[:, None]
    past_scores = jnp.where(live[:, None, :], past_scores, -jnp.inf)
    visible = ancestry(parents)
    seen = jnp.broadcast_to(
        visible[:, None], (slots, heads_loc, tree_size, tree_size)
    ).reshape(slots, heads_loc * tree_size, tree_size)
    tree_scores = (
        jnp.einsum("rnd,rkd->rnk", spread_q, key_new, preferred_element_type=jnp.float32)
        * score_scale
    )
    tree_scores = jnp.where(seen, tree_scores, -jnp.inf)
    highest = jnp.maximum(jnp.max(past_scores, axis=2), jnp.max(tree_scores, axis=2))
    past_weights = jnp.exp(past_scores - highest[..., None])
    tree_weights = jnp.exp(tree_scores - highest[..., None])
    denominator = jnp.sum(past_weights, axis=2) + jnp.sum(tree_weights, axis=2)
    mixed = jnp.einsum(
        "rnk,rkd->rnd",
        past_weights.astype(jnp.bfloat16),
        cache_value,
        preferred_element_type=jnp.float32,
    ) + jnp.einsum(
        "rnk,rkd->rnd",
        tree_weights.astype(jnp.bfloat16),
        value_new,
        preferred_element_type=jnp.float32,
    )
    mixed = (mixed / denominator[..., None]).reshape(slots, heads_loc, tree_size, qwidth)
    attention = jnp.sum(
        jnp.where(head_mask[None, :, None, :], mixed, 0.0), axis=1
    ).astype(jnp.bfloat16)
    attention_rows = attention.reshape(slots * tree_size, qwidth)
    rows_all = slots * tree_size
    quarter = rows_all // n_tp
    dslice = model_width // n_tp
    halves = tree_size // quarter
    acc_rows = accept.shape[1]
    own_slot = tp_id // halves
    node_off = (tp_id % halves) * quarter
    partial_out = jnp.dot(
        attention_rows, out_weight, preferred_element_type=jnp.float32
    ).astype(jnp.bfloat16)
    blocks = partial_out.reshape(n_tp, quarter, model_width)
    summed = lax.dynamic_index_in_dim(blocks, tp_id, 0, keepdims=False).astype(jnp.float32)
    for shift in range(1, n_tp):
        outbound = lax.dynamic_index_in_dim(blocks, (tp_id + shift) % n_tp, 0, keepdims=False)
        summed = summed + lax.ppermute(
            outbound, "tp", [(t, (t + shift) % n_tp) for t in range(n_tp)]
        ).astype(jnp.float32)
    flat_stream = stream.reshape(rows_all, model_width)
    own_stream = lax.dynamic_slice_in_dim(flat_stream, tp_id * quarter, quarter, 0)
    post_rows = (own_stream.astype(jnp.float32) + summed).astype(jnp.bfloat16)
    post_float = post_rows.astype(jnp.float32)
    square = jnp.sum(post_float * post_float, axis=1)
    inverse = lax.rsqrt(square / model_width + EPS)
    normed = (post_float * inverse[:, None] * norm_gain[None, :]).astype(jnp.bfloat16)
    accept_own = lax.dynamic_slice_in_dim(
        lax.dynamic_index_in_dim(accept, own_slot, 0, keepdims=False), node_off, quarter, 1
    )
    picked_rows = jnp.dot(
        accept_own.astype(jnp.bfloat16), post_rows, preferred_element_type=jnp.float32
    ).astype(jnp.bfloat16)
    n_slots = dealing.shape[0]
    slot_ids = jnp.arange(n_slots, dtype=jnp.int32)
    picked_parts = picked_rows.reshape(acc_rows, n_tp, dslice).transpose(1, 0, 2)
    parts_in = lax.all_to_all(picked_parts, "tp", split_axis=0, concat_axis=0, tiled=True)
    plane_slot = jnp.arange(n_tp, dtype=jnp.int32) // halves
    local_slots = jnp.arange(slots, dtype=jnp.int32)
    compact = jnp.einsum(
        "lt,tad->lad",
        (plane_slot[None, :] == local_slots[:, None]).astype(jnp.bfloat16),
        parts_in,
        preferred_element_type=jnp.float32,
    ).astype(jnp.bfloat16)
    my_slots = req_id * slots + local_slots
    my_requests = jnp.sum(
        jnp.where(slot_ids[None, :] == my_slots[:, None], dealing[None, :], 0), axis=1
    )
    dest_ids = jnp.arange(n_req, dtype=jnp.int32)
    compact_out = jnp.where(
        ((my_requests // slots)[None, :] == dest_ids[:, None])[:, :, None, None],
        compact[None],
        jnp.zeros((), compact.dtype),
    )
    compact_in = lax.all_to_all(
        compact_out.reshape(n_req, slots * acc_rows, dslice),
        "req",
        split_axis=0,
        concat_axis=0,
        tiled=True,
    )
    all_rows = lax.all_gather(normed, "req", axis=0, tiled=True)
    vocab_loc = head_weight.shape[0]
    wanted_rows = lax.dynamic_slice_in_dim(
        candidate.reshape(n_req, rows_all), tp_id * quarter, quarter, 1
    ).reshape(-1)
    vocab_ids = req_id * vocab_loc + jnp.arange(vocab_loc, dtype=jnp.int32)
    logits = lax.dot_general(
        all_rows, head_weight, (((1,), (1,)), ((), ())), preferred_element_type=jnp.float32
    )
    serving_all = jnp.sum(
        jnp.where(dealing[None, :] == slot_ids[:, None], slot_ids[None, :], 0), axis=1
    )
    own_requests = req_id * slots + jnp.arange(slots, dtype=jnp.int32)
    own_serving = jnp.sum(
        jnp.where(dealing[None, :] == own_requests[:, None], slot_ids[None, :], 0), axis=1
    )
    routed = dealing[None, :] == own_requests[:, None]
    accepted_state = jnp.einsum(
        "ks,sad->kad",
        routed.astype(jnp.bfloat16),
        compact_in.reshape(n_slots, acc_rows, dslice),
        preferred_element_type=jnp.float32,
    ).astype(jnp.bfloat16)
    row_max, row_sum, picked = vocab_stats(logits, vocab_ids, wanted_rows, 1)
    local_stats = jnp.stack([row_max, row_sum, picked]).reshape(3, n_req, quarter)
    local_stats = local_stats.transpose(1, 0, 2)
    dest_blocks = (serving_all // slots).reshape(n_req, 1, slots)
    dest_blocks = jnp.broadcast_to(dest_blocks, (n_req, n_tp, slots)).reshape(-1)
    block_ids = jnp.arange(n_req, dtype=jnp.int32)
    outgoing = jnp.sum(
        jnp.where(
            (dest_blocks[:, None] == block_ids[None, :])[:, :, None, None],
            local_stats[None],
            0.0,
        ),
        axis=1,
    ).reshape(n_req * n_tp, slots, 3, quarter)
    chunk = slots * 3 * quarter
    tile = 8 * 128
    padded = jnp.pad(
        outgoing.reshape(n_req * n_tp, chunk), ((0, 0), (0, -chunk % tile))
    ).reshape(n_req * n_tp, -1, 128)
    incoming = lax.all_to_all(
        padded, ("req", "tp"), split_axis=0, concat_axis=0, tiled=True
    ).reshape(n_req * n_tp, -1)[:, :chunk].reshape(n_req, n_tp, slots, 3, quarter)
    plane_of = (own_serving % slots)[:, None] * halves + jnp.arange(halves, dtype=jnp.int32)[None, :]
    plane_ids = jnp.arange(n_tp, dtype=jnp.int32)
    chosen = jnp.sum(
        jnp.where(
            (plane_of[:, :, None] == plane_ids[None, None, :])[None, :, :, :, None, None],
            incoming.transpose(0, 2, 1, 3, 4)[:, :, None],
            0.0,
        ),
        axis=3,
    )
    joint_max = jnp.max(chosen[:, :, :, 0], axis=0)
    joint_sum = jnp.sum(chosen[:, :, :, 1] * jnp.exp(chosen[:, :, :, 0] - joint_max[None]), axis=0)
    joint_pick = jnp.sum(chosen[:, :, :, 2], axis=0)
    target_logprob = (joint_pick - joint_max - jnp.log(joint_sum)).reshape(slots, tree_size)
    return (target_logprob, accepted_state)


def solution(mesh):
    placed = (
        P("req", None, None),
        P("req", None, "tp"),
        P("req", None, "tp"),
        P("req", None, "tp"),
        P("req", None, "tp"),
        P("req", None, "tp"),
        P("req"),
        P("req", None),
        P("req", None, None),
        P("tp", None),
        P(),
        P("req", None),
        P(),
        P(),
    )
    return jax.shard_map(
        local,
        mesh=mesh,
        in_specs=placed,
        out_specs=(P("req", None), P("req", None, "tp")),
        check_vma=False,
    )
```

```python
import jax
import jax.numpy as jnp
from jax import lax
from jax.sharding import PartitionSpec as P

HD = 224
ACC = 8


EPS = 1e-05
HIGH = lax.Precision.HIGHEST
block_limit = 512


def combined_all(value, axis, join):
    pieces = jax.tree.map(lambda part: lax.all_gather(part, axis), value)
    head = jax.tree.map(lambda part: part[0], pieces)
    tail = jax.tree.map(lambda part: part[1:], pieces)
    subtotal, _ = lax.scan(lambda subtotal, share: (join(subtotal, share), None), head, tail)
    return subtotal


def ancestry(parents):
    node_count = parents.shape[-1]
    node_ids = jnp.arange(node_count, dtype=jnp.int32)
    stride_map = (parents[..., :, None] == node_ids).astype(jnp.float32)
    reached = jnp.broadcast_to(jnp.eye(node_count, dtype=jnp.float32), stride_map.shape) > 0.5
    for doubling in range((ACC - 1).bit_length()):
        further = lax.optimization_barrier(
            jnp.einsum("rtk,rku->rtu", reached.astype(jnp.float32), stride_map, precision=HIGH)
        )
        reached = jnp.logical_or(reached, further > 0.5)
        stride_map = jnp.einsum("rtk,rku->rtu", stride_map, stride_map, precision=HIGH)
    return reached


def combine_stats(earlier, later):
    joint_max = jnp.maximum(earlier[0], later[0])
    joint_sum = earlier[1] * jnp.exp(earlier[0] - joint_max) + later[1] * jnp.exp(
        later[0] - joint_max
    )
    return (joint_max, joint_sum, earlier[2] + later[2])


def vocab_stats(logits, vocab_ids, wanted, along):
    row_max = jnp.max(logits, axis=along)
    row_sum = jnp.sum(jnp.exp(logits - jnp.expand_dims(row_max, along)), axis=along)
    matches = jnp.expand_dims(vocab_ids, 1 - along) == jnp.expand_dims(wanted, along)
    picked = jnp.sum(jnp.where(matches, logits, 0.0), axis=along)
    return (row_max, row_sum, picked)


def local(
    stream,
    queries,
    key_new,
    value_new,
    cache_key,
    cache_value,
    cache_length,
    parents,
    accept,
    out_weight,
    norm_gain,
    head_weight,
    candidate,
    dealing,
):
    slots, tree_size, qwidth = queries.shape
    model_width = stream.shape[2]
    heads_loc = qwidth // HD
    n_tp = lax.axis_size("tp")
    n_req = lax.axis_size("req")
    tp_id = lax.axis_index("tp")
    req_id = lax.axis_index("req")
    score_scale = HD ** (-0.5)
    cache_cap = cache_key.shape[1]
    column_head = jnp.arange(qwidth, dtype=jnp.int32) // HD
    head_mask = column_head[None, :] == jnp.arange(heads_loc, dtype=jnp.int32)[:, None]
    spread_q = jnp.where(
        head_mask[None, :, None, :], queries[:, None, :, :], jnp.zeros((), queries.dtype)
    ).reshape(slots, heads_loc * tree_size, qwidth)
    past_scores = (
        jnp.einsum("rnd,rkd->rnk", spread_q, cache_key, preferred_element_type=jnp.float32)
        * score_scale
    )
    live = jnp.arange(cache_cap, dtype=jnp.int32)[None, :] < cache_length[:, None]
    past_scores = jnp.where(live[:, None, :], past_scores, -jnp.inf)
    visible = ancestry(parents)
    seen = jnp.broadcast_to(
        visible[:, None], (slots, heads_loc, tree_size, tree_size)
    ).reshape(slots, heads_loc * tree_size, tree_size)
    tree_scores = (
        jnp.einsum("rnd,rkd->rnk", spread_q, key_new, preferred_element_type=jnp.float32)
        * score_scale
    )
    tree_scores = jnp.where(seen, tree_scores, -jnp.inf)
    highest = jnp.maximum(jnp.max(past_scores, axis=2), jnp.max(tree_scores, axis=2))
    past_weights = jnp.exp(past_scores - highest[..., None])
    tree_weights = jnp.exp(tree_scores - highest[..., None])
    denominator = jnp.sum(past_weights, axis=2) + jnp.sum(tree_weights, axis=2)
    mixed = jnp.einsum(
        "rnk,rkd->rnd",
        past_weights.astype(jnp.bfloat16),
        cache_value,
        preferred_element_type=jnp.float32,
    ) + jnp.einsum(
        "rnk,rkd->rnd",
        tree_weights.astype(jnp.bfloat16),
        value_new,
        preferred_element_type=jnp.float32,
    )
    mixed = (mixed / denominator[..., None]).reshape(slots, heads_loc, tree_size, qwidth)
    attention = jnp.sum(
        jnp.where(head_mask[None, :, None, :], mixed, 0.0), axis=1
    ).astype(jnp.bfloat16)
    attention_rows = attention.reshape(slots * tree_size, qwidth)
    rows_all = slots * tree_size
    quarter = rows_all // n_tp
    dslice = model_width // n_tp
    halves = tree_size // quarter
    acc_rows = accept.shape[1]
    own_slot = tp_id // halves
    node_off = (tp_id % halves) * quarter
    partial_out = jnp.dot(
        attention_rows, out_weight, preferred_element_type=jnp.float32
    ).astype(jnp.bfloat16)
    blocks = partial_out.reshape(n_tp, quarter, model_width)
    summed = lax.dynamic_index_in_dim(blocks, tp_id, 0, keepdims=False).astype(jnp.float32)
    for shift in range(1, n_tp):
        outbound = lax.dynamic_index_in_dim(blocks, (tp_id + shift) % n_tp, 0, keepdims=False)
        summed = summed + lax.ppermute(
            outbound, "tp", [(t, (t + shift) % n_tp) for t in range(n_tp)]
        ).astype(jnp.float32)
    flat_stream = stream.reshape(rows_all, model_width)
    own_stream = lax.dynamic_slice_in_dim(flat_stream, tp_id * quarter, quarter, 0)
    post_rows = (own_stream.astype(jnp.float32) + summed).astype(jnp.bfloat16)
    post_float = post_rows.astype(jnp.float32)
    square = jnp.sum(post_float * post_float, axis=1)
    inverse = lax.rsqrt(square / model_width + EPS)
    normed = (post_float * inverse[:, None] * norm_gain[None, :]).astype(jnp.bfloat16)
    accept_own = lax.dynamic_slice_in_dim(
        lax.dynamic_index_in_dim(accept, own_slot, 0, keepdims=False), node_off, quarter, 1
    )
    picked_rows = jnp.dot(
        accept_own.astype(jnp.bfloat16), post_rows, preferred_element_type=jnp.float32
    ).astype(jnp.bfloat16)
    n_slots = dealing.shape[0]
    slot_ids = jnp.arange(n_slots, dtype=jnp.int32)
    picked_parts = picked_rows.reshape(acc_rows, n_tp, dslice).transpose(1, 0, 2)
    parts_in = lax.all_to_all(picked_parts, "tp", split_axis=0, concat_axis=0, tiled=True)
    plane_slot = jnp.arange(n_tp, dtype=jnp.int32) // halves
    local_slots = jnp.arange(slots, dtype=jnp.int32)
    compact = jnp.einsum(
        "lt,tad->lad",
        (plane_slot[None, :] == local_slots[:, None]).astype(jnp.bfloat16),
        parts_in,
        preferred_element_type=jnp.float32,
    ).astype(jnp.bfloat16)
    my_slots = req_id * slots + local_slots
    my_requests = jnp.sum(
        jnp.where(slot_ids[None, :] == my_slots[:, None], dealing[None, :], 0), axis=1
    )
    dest_ids = jnp.arange(n_req, dtype=jnp.int32)
    compact_out = jnp.where(
        ((my_requests // slots)[None, :] == dest_ids[:, None])[:, :, None, None],
        compact[None],
        jnp.zeros((), compact.dtype),
    )
    compact_in = lax.all_to_all(
        compact_out.reshape(n_req, slots * acc_rows, dslice),
        "req",
        split_axis=0,
        concat_axis=0,
        tiled=True,
    )
    all_rows = lax.all_gather(normed, "req", axis=0, tiled=True)
    vocab_loc = head_weight.shape[0]
    wanted_rows = lax.dynamic_slice_in_dim(
        candidate.reshape(n_req, rows_all), tp_id * quarter, quarter, 1
    ).reshape(-1)
    vocab_ids = req_id * vocab_loc + jnp.arange(vocab_loc, dtype=jnp.int32)
    split_at = (vocab_loc // 2) // 16 * 16
    part_stats = []
    for lo, hi in ((0, split_at), (split_at, vocab_loc)):
        part_logits = lax.dot_general(
            all_rows,
            head_weight[lo:hi],
            (((1,), (1,)), ((), ())),
            preferred_element_type=jnp.float32,
        )
        part_stats.append(vocab_stats(part_logits, vocab_ids[lo:hi], wanted_rows, 1))
    serving_all = jnp.sum(
        jnp.where(dealing[None, :] == slot_ids[:, None], slot_ids[None, :], 0), axis=1
    )
    own_requests = req_id * slots + jnp.arange(slots, dtype=jnp.int32)
    own_serving = jnp.sum(
        jnp.where(dealing[None, :] == own_requests[:, None], slot_ids[None, :], 0), axis=1
    )
    routed = dealing[None, :] == own_requests[:, None]
    accepted_state = jnp.einsum(
        "ks,sad->kad",
        routed.astype(jnp.bfloat16),
        compact_in.reshape(n_slots, acc_rows, dslice),
        preferred_element_type=jnp.float32,
    ).astype(jnp.bfloat16)
    row_max, row_sum, picked = combine_stats(part_stats[0], part_stats[1])
    local_stats = jnp.stack([row_max, row_sum, picked]).reshape(3, n_req, quarter)
    local_stats = local_stats.transpose(1, 0, 2)
    dest_blocks = (serving_all // slots).reshape(n_req, 1, slots)
    dest_blocks = jnp.broadcast_to(dest_blocks, (n_req, n_tp, slots)).reshape(-1)
    block_ids = jnp.arange(n_req, dtype=jnp.int32)
    outgoing = jnp.sum(
        jnp.where(
            (dest_blocks[:, None] == block_ids[None, :])[:, :, None, None],
            local_stats[None],
            0.0,
        ),
        axis=1,
    ).reshape(n_req * n_tp, slots, 3, quarter)
    incoming = lax.all_to_all(
        outgoing.reshape(n_req * n_tp, slots * 3 * quarter),
        ("req", "tp"),
        split_axis=0,
        concat_axis=0,
        tiled=True,
    ).reshape(n_req, n_tp, slots, 3, quarter)
    plane_of = (own_serving % slots)[:, None] * halves + jnp.arange(halves, dtype=jnp.int32)[None, :]
    plane_ids = jnp.arange(n_tp, dtype=jnp.int32)
    chosen = jnp.sum(
        jnp.where(
            (plane_of[:, :, None] == plane_ids[None, None, :])[None, :, :, :, None, None],
            incoming.transpose(0, 2, 1, 3, 4)[:, :, None],
            0.0,
        ),
        axis=3,
    )
    joint_max = jnp.max(chosen[:, :, :, 0], axis=0)
    joint_sum = jnp.sum(chosen[:, :, :, 1] * jnp.exp(chosen[:, :, :, 0] - joint_max[None]), axis=0)
    joint_pick = jnp.sum(chosen[:, :, :, 2], axis=0)
    target_logprob = (joint_pick - joint_max - jnp.log(joint_sum)).reshape(slots, tree_size)
    return (target_logprob, accepted_state)


def solution(mesh):
    placed = (
        P("req", None, None),
        P("req", None, "tp"),
        P("req", None, "tp"),
        P("req", None, "tp"),
        P("req", None, "tp"),
        P("req", None, "tp"),
        P("req"),
        P("req", None),
        P("req", None, None),
        P("tp", None),
        P(),
        P("req", None),
        P(),
        P(),
    )
    return jax.shard_map(
        local,
        mesh=mesh,
        in_specs=placed,
        out_specs=(P("req", None), P("req", None, "tp")),
        check_vma=False,
    )
```

```python
import jax
import jax.numpy as jnp
from jax import lax
from jax.sharding import PartitionSpec as P

HD = 224
ACC = 8


EPS = 1e-05
HIGH = lax.Precision.HIGHEST
block_limit = 512


def combined_all(value, axis, join):
    pieces = jax.tree.map(lambda part: lax.all_gather(part, axis), value)
    head = jax.tree.map(lambda part: part[0], pieces)
    tail = jax.tree.map(lambda part: part[1:], pieces)
    subtotal, _ = lax.scan(lambda subtotal, share: (join(subtotal, share), None), head, tail)
    return subtotal


def ancestry(parents):
    node_count = parents.shape[-1]
    node_ids = jnp.arange(node_count, dtype=jnp.int32)
    stride_map = (parents[..., :, None] == node_ids).astype(jnp.float32)
    reached = jnp.broadcast_to(jnp.eye(node_count, dtype=jnp.float32), stride_map.shape) > 0.5
    for doubling in range((ACC - 1).bit_length()):
        further = lax.optimization_barrier(
            jnp.einsum("rtk,rku->rtu", reached.astype(jnp.float32), stride_map, precision=HIGH)
        )
        reached = jnp.logical_or(reached, further > 0.5)
        stride_map = jnp.einsum("rtk,rku->rtu", stride_map, stride_map, precision=HIGH)
    return reached


def combine_stats(earlier, later):
    joint_max = jnp.maximum(earlier[0], later[0])
    joint_sum = earlier[1] * jnp.exp(earlier[0] - joint_max) + later[1] * jnp.exp(
        later[0] - joint_max
    )
    return (joint_max, joint_sum, earlier[2] + later[2])


def vocab_stats(logits, vocab_ids, wanted, along):
    row_max = jnp.max(logits, axis=along)
    row_sum = jnp.sum(jnp.exp(logits - jnp.expand_dims(row_max, along)), axis=along)
    matches = jnp.expand_dims(vocab_ids, 1 - along) == jnp.expand_dims(wanted, along)
    picked = jnp.sum(jnp.where(matches, logits, 0.0), axis=along)
    return (row_max, row_sum, picked)


def local(
    stream,
    queries,
    key_new,
    value_new,
    cache_key,
    cache_value,
    cache_length,
    parents,
    accept,
    out_weight,
    norm_gain,
    head_weight,
    candidate,
    dealing,
):
    slots, tree_size, qwidth = queries.shape
    model_width = stream.shape[2]
    heads_loc = qwidth // HD
    n_tp = lax.axis_size("tp")
    n_req = lax.axis_size("req")
    tp_id = lax.axis_index("tp")
    req_id = lax.axis_index("req")
    score_scale = HD ** (-0.5)
    cache_cap = cache_key.shape[1]
    column_head = jnp.arange(qwidth, dtype=jnp.int32) // HD
    head_mask = column_head[None, :] == jnp.arange(heads_loc, dtype=jnp.int32)[:, None]
    spread_q = jnp.where(
        head_mask[None, :, None, :], queries[:, None, :, :], jnp.zeros((), queries.dtype)
    ).reshape(slots, heads_loc * tree_size, qwidth)
    past_scores = (
        jnp.einsum("rnd,rkd->rnk", spread_q, cache_key, preferred_element_type=jnp.float32)
        * score_scale
    )
    live = jnp.arange(cache_cap, dtype=jnp.int32)[None, :] < cache_length[:, None]
    past_scores = jnp.where(live[:, None, :], past_scores, -jnp.inf)
    visible = ancestry(parents)
    seen = jnp.broadcast_to(
        visible[:, None], (slots, heads_loc, tree_size, tree_size)
    ).reshape(slots, heads_loc * tree_size, tree_size)
    tree_scores = (
        jnp.einsum("rnd,rkd->rnk", spread_q, key_new, preferred_element_type=jnp.float32)
        * score_scale
    )
    tree_scores = jnp.where(seen, tree_scores, -jnp.inf)
    highest = jnp.maximum(jnp.max(past_scores, axis=2), jnp.max(tree_scores, axis=2))
    past_weights = jnp.exp(past_scores - highest[..., None])
    tree_weights = jnp.exp(tree_scores - highest[..., None])
    denominator = jnp.sum(past_weights, axis=2) + jnp.sum(tree_weights, axis=2)
    mixed = jnp.einsum(
        "rnk,rkd->rnd",
        past_weights.astype(jnp.bfloat16),
        cache_value,
        preferred_element_type=jnp.float32,
    ) + jnp.einsum(
        "rnk,rkd->rnd",
        tree_weights.astype(jnp.bfloat16),
        value_new,
        preferred_element_type=jnp.float32,
    )
    mixed = (mixed / denominator[..., None]).reshape(slots, heads_loc, tree_size, qwidth)
    attention = jnp.sum(
        jnp.where(head_mask[None, :, None, :], mixed, 0.0), axis=1
    ).astype(jnp.bfloat16)
    attention_rows = attention.reshape(slots * tree_size, qwidth)
    rows_all = slots * tree_size
    quarter = rows_all // n_tp
    dslice = model_width // n_tp
    halves = tree_size // quarter
    acc_rows = accept.shape[1]
    own_slot = tp_id // halves
    node_off = (tp_id % halves) * quarter
    partial_out = jnp.dot(
        attention_rows, out_weight, preferred_element_type=jnp.float32
    ).astype(jnp.bfloat16)
    blocks = partial_out.reshape(n_tp, quarter, model_width)
    summed = lax.dynamic_index_in_dim(blocks, tp_id, 0, keepdims=False).astype(jnp.float32)
    for shift in range(1, n_tp):
        outbound = lax.dynamic_index_in_dim(blocks, (tp_id + shift) % n_tp, 0, keepdims=False)
        summed = summed + lax.ppermute(
            outbound, "tp", [(t, (t + shift) % n_tp) for t in range(n_tp)]
        ).astype(jnp.float32)
    flat_stream = stream.reshape(rows_all, model_width)
    own_stream = lax.dynamic_slice_in_dim(flat_stream, tp_id * quarter, quarter, 0)
    post_rows = (own_stream.astype(jnp.float32) + summed).astype(jnp.bfloat16)
    post_float = post_rows.astype(jnp.float32)
    square = jnp.sum(post_float * post_float, axis=1)
    inverse = lax.rsqrt(square / model_width + EPS)
    normed = (post_float * inverse[:, None] * norm_gain[None, :]).astype(jnp.bfloat16)
    accept_own = lax.dynamic_slice_in_dim(
        lax.dynamic_index_in_dim(accept, own_slot, 0, keepdims=False), node_off, quarter, 1
    )
    picked_rows = jnp.dot(
        accept_own.astype(jnp.bfloat16), post_rows, preferred_element_type=jnp.float32
    ).astype(jnp.bfloat16)
    n_slots = dealing.shape[0]
    slot_ids = jnp.arange(n_slots, dtype=jnp.int32)
    picked_parts = picked_rows.reshape(acc_rows, n_tp, dslice).transpose(1, 0, 2)
    parts_in = lax.all_to_all(picked_parts, "tp", split_axis=0, concat_axis=0, tiled=True)
    plane_slot = jnp.arange(n_tp, dtype=jnp.int32) // halves
    local_slots = jnp.arange(slots, dtype=jnp.int32)
    compact = jnp.einsum(
        "lt,tad->lad",
        (plane_slot[None, :] == local_slots[:, None]).astype(jnp.bfloat16),
        parts_in,
        preferred_element_type=jnp.float32,
    ).astype(jnp.bfloat16)
    my_slots = req_id * slots + local_slots
    my_requests = jnp.sum(
        jnp.where(slot_ids[None, :] == my_slots[:, None], dealing[None, :], 0), axis=1
    )
    dest_ids = jnp.arange(n_req, dtype=jnp.int32)
    compact_out = jnp.where(
        ((my_requests // slots)[None, :] == dest_ids[:, None])[:, :, None, None],
        compact[None],
        jnp.zeros((), compact.dtype),
    )
    compact_in = lax.all_to_all(
        compact_out.reshape(n_req, slots * acc_rows, dslice),
        "req",
        split_axis=0,
        concat_axis=0,
        tiled=True,
    )
    all_rows = lax.all_gather(normed, "req", axis=0, tiled=True)
    vocab_loc = head_weight.shape[0]
    wanted_rows = lax.dynamic_slice_in_dim(
        candidate.reshape(n_req, rows_all), tp_id * quarter, quarter, 1
    ).reshape(-1)
    vocab_ids = req_id * vocab_loc + jnp.arange(vocab_loc, dtype=jnp.int32)
    bounds = [min(vocab_loc, k * 256) for k in range(-(-vocab_loc // 256))] + [vocab_loc]
    part_stats = []
    for lo, hi in zip(bounds[:-1], bounds[1:]):
        part_logits = lax.dot_general(
            all_rows,
            head_weight[lo:hi],
            (((1,), (1,)), ((), ())),
            preferred_element_type=jnp.float32,
        )
        part_stats.append(vocab_stats(part_logits, vocab_ids[lo:hi], wanted_rows, 1))
    serving_all = jnp.sum(
        jnp.where(dealing[None, :] == slot_ids[:, None], slot_ids[None, :], 0), axis=1
    )
    own_requests = req_id * slots + jnp.arange(slots, dtype=jnp.int32)
    own_serving = jnp.sum(
        jnp.where(dealing[None, :] == own_requests[:, None], slot_ids[None, :], 0), axis=1
    )
    routed = dealing[None, :] == own_requests[:, None]
    accepted_state = jnp.einsum(
        "ks,sad->kad",
        routed.astype(jnp.bfloat16),
        compact_in.reshape(n_slots, acc_rows, dslice),
        preferred_element_type=jnp.float32,
    ).astype(jnp.bfloat16)
    row_max, row_sum, picked = part_stats[0]
    for more in part_stats[1:]:
        row_max, row_sum, picked = combine_stats((row_max, row_sum, picked), more)
    local_stats = jnp.stack([row_max, row_sum, picked]).reshape(3, n_req, quarter)
    local_stats = local_stats.transpose(1, 0, 2)
    dest_blocks = (serving_all // slots).reshape(n_req, 1, slots)
    dest_blocks = jnp.broadcast_to(dest_blocks, (n_req, n_tp, slots)).reshape(-1)
    block_ids = jnp.arange(n_req, dtype=jnp.int32)
    outgoing = jnp.sum(
        jnp.where(
            (dest_blocks[:, None] == block_ids[None, :])[:, :, None, None],
            local_stats[None],
            0.0,
        ),
        axis=1,
    ).reshape(n_req * n_tp, slots, 3, quarter)
    incoming = lax.all_to_all(
        outgoing.reshape(n_req * n_tp, slots * 3 * quarter),
        ("req", "tp"),
        split_axis=0,
        concat_axis=0,
        tiled=True,
    ).reshape(n_req, n_tp, slots, 3, quarter)
    plane_of = (own_serving % slots)[:, None] * halves + jnp.arange(halves, dtype=jnp.int32)[None, :]
    plane_ids = jnp.arange(n_tp, dtype=jnp.int32)
    chosen = jnp.sum(
        jnp.where(
            (plane_of[:, :, None] == plane_ids[None, None, :])[None, :, :, :, None, None],
            incoming.transpose(0, 2, 1, 3, 4)[:, :, None],
            0.0,
        ),
        axis=3,
    )
    joint_max = jnp.max(chosen[:, :, :, 0], axis=0)
    joint_sum = jnp.sum(chosen[:, :, :, 1] * jnp.exp(chosen[:, :, :, 0] - joint_max[None]), axis=0)
    joint_pick = jnp.sum(chosen[:, :, :, 2], axis=0)
    target_logprob = (joint_pick - joint_max - jnp.log(joint_sum)).reshape(slots, tree_size)
    return (target_logprob, accepted_state)


def solution(mesh):
    placed = (
        P("req", None, None),
        P("req", None, "tp"),
        P("req", None, "tp"),
        P("req", None, "tp"),
        P("req", None, "tp"),
        P("req", None, "tp"),
        P("req"),
        P("req", None),
        P("req", None, None),
        P("tp", None),
        P(),
        P("req", None),
        P(),
        P(),
    )
    return jax.shard_map(
        local,
        mesh=mesh,
        in_specs=placed,
        out_specs=(P("req", None), P("req", None, "tp")),
        check_vma=False,
    )
```
